128 devices in a mesh: seg: 16 (over x, y_lo, core), dp: 8 (over y_hi, z).
Axes of the slice: x: 4, y: 4 (y_hi: 2, y_lo: 2; y = y_hi * 2 + y_lo), z: 4, core: 2. Of those that a mesh axis runs over, the one named last changes fastest.
Arguments:
- hidden: bfloat16 [8, 5120, 4096], P('dp', 'seg'), may hold values from -6 to 6
- norm_gain: bfloat16 [4096], replicated, may hold values from 0.5 to 1.5
- value_weight: bfloat16 [4096, 2048], replicated, may hold values from -0.09375 to 0.09375
- queries: bfloat16 [8, 5120, 2048], P('dp', 'seg'), may hold values from -100 to 100
- token_keys: bfloat16 [8, 5120, 2048], P('dp', 'seg'), may hold values from -5 to 5
- summary_keys: bfloat16 [8, 800, 2048], P('dp', 'seg'), may hold values from -5 to 5
- output_grad: bfloat16 [8, 5120, 2048], P('dp', 'seg'), may hold values from -6 to 6
Outputs:
- grad_hidden: bfloat16 [8, 5120, 4096], P('dp', 'seg')
- summary_grads: float32 [8, 800, 2048], P('dp', 'seg')
- grad_weight: float32 [4096, 2048], P(('seg', 'dp'))
- grad_gain: float32 [4096], P(('seg', 'dp'))
The draws below stay inside these ranges and needn't reach their ends.
All inputs are finite; a program needn't handle non-finite values.
Results may differ from the reference program's by a relative error of at most 0.0058.
Values sent between devices are 32-bit elements; how exact they have to be, the bound alone decides.
No kernel may reach another device: no remote copies, remote signals or barrier semaphores. Data moves between devices by JAX's collectives and lax.ppermute only.
A program may use at most 192 MiB of HBM per device.

```python
import math
import jax
import jax.numpy as jnp
from jax import lax

D = 4096
HEADS = 16
HEAD_DIM = 128
SUMMARY = 50
ROWS = 320
HD = 2048
TRACE_TOTAL = 8
SEQ = 5120
SUMS = 800
N_SEG = 16


def key_values(key):
    normal_keys = jax.random.normal(jax.random.fold_in(key, 101), (TRACE_TOTAL, SEQ, HD), jnp.float32)
    return jnp.clip(normal_keys, -5.0, 5.0)


def summary_values(key):
    normal_keys = jax.random.normal(jax.random.fold_in(key, 303), (TRACE_TOTAL, SUMS, HD), jnp.float32)
    return jnp.clip(normal_keys, -5.0, 5.0)


def draw_token_keys(key, part):
    return key_values(key).astype(jnp.bfloat16)


def draw_summary_keys(key, part):
    return summary_values(key).astype(jnp.bfloat16)


def draw_queries(key, part):
    segment_list = SEQ // ROWS
    drawn = jax.random.normal(jax.random.fold_in(key, 202), (TRACE_TOTAL, SEQ, HD), jnp.float32)
    drawn = jnp.clip(drawn, -5.0, 5.0)
    head_draw = jax.random.uniform(jax.random.fold_in(key, 404), (TRACE_TOTAL, 1, 1, HEADS, 1), jnp.float32)
    persistent_factor = head_draw < 0.5
    spike_sample = jax.random.uniform(jax.random.fold_in(key, 505), (TRACE_TOTAL, segment_list, 1, 1, 1), jnp.float32)
    spike_factor = spike_sample < 0.15
    slack_amount = jnp.where(persistent_factor, jnp.where(spike_factor, 1.2, 5.6), 0.6)
    strength_slot = (math.log(ROWS + SUMMARY) + slack_amount) / math.sqrt(HEAD_DIM)
    summary_f = summary_values(key).astype(jnp.bfloat16).astype(jnp.float32)
    summary_f = summary_f.reshape(TRACE_TOTAL, segment_list, SUMMARY, HEADS, HEAD_DIM)
    aligned = (strength_slot * summary_f).reshape(TRACE_TOTAL, segment_list, SUMMARY, HD)
    blocks = drawn.reshape(TRACE_TOTAL, segment_list, ROWS, HD)
    blocks = jnp.concatenate([blocks[:, :, :ROWS - SUMMARY], aligned], axis=2)
    return blocks.reshape(TRACE_TOTAL, SEQ, HD).astype(jnp.bfloat16)


def shard_levels(own_key, shape, pieces, least, high):
    def one(dim, parts):
        draws = jax.random.uniform(jax.random.fold_in(jax.random.fold_in(own_key, 6), dim), (parts,), jnp.float32, least / len(pieces), high / len(pieces))
        return jnp.repeat(jnp.exp(draws), shape[dim] // parts).reshape((-1,) + (1,) * (len(shape) - dim - 1))

    gain = one(*pieces[0])
    for cut in pieces[1:]:
        gain = gain * one(*cut)
    return gain


def bell_draw(own_key, extent, width, reach, pieces=(), dtype=jnp.bfloat16):
    values = width * jax.random.normal(own_key, extent, jnp.float32)
    if pieces:
        values = values * shard_levels(own_key, extent, pieces, -0.22, 0.18)
    return jnp.clip(values, -reach, reach).astype(dtype)


def setup_inputs(seed: int = 0) -> dict:
    key_of = jax.random.split(jax.random.key(seed), 8)
    hidden = bell_draw(key_of[0], (TRACE_TOTAL, SEQ, D), 1.0, 6.0, ((0, 8), (1, 16)))
    norm_gain = jnp.clip(1.0 + 0.1 * jax.random.normal(key_of[1], (D,), jnp.float32), 0.5, 1.5).astype(jnp.bfloat16)
    value_weight = bell_draw(key_of[2], (D, HD), D ** -0.5, 0.09375)
    queries = draw_queries(jax.random.fold_in(key_of[7], 71), 0)
    token_keys = draw_token_keys(jax.random.fold_in(key_of[7], 71), 0)
    summary_keys = draw_summary_keys(jax.random.fold_in(key_of[7], 71), 0)
    output_grad = bell_draw(key_of[6], (TRACE_TOTAL, SEQ, HD), 1.0, 6.0, ((0, 8), (1, 16)))
    return {"hidden": hidden, "norm_gain": norm_gain, "value_weight": value_weight, "queries": queries, "token_keys": token_keys, "summary_keys": summary_keys, "output_grad": output_grad}


def mixing_of(query_rows, key_rows, summary_rows):
    trace_count = query_rows.shape[0]
    query_heads = query_rows.astype(jnp.float32).reshape(trace_count, ROWS, HEADS, HEAD_DIM)
    all_keys = jnp.concatenate([summary_rows, key_rows], axis=1).astype(jnp.float32)
    all_keys = all_keys.reshape(trace_count, SUMMARY + ROWS, HEADS, HEAD_DIM)
    scores = jnp.einsum('trhd,tkhd->thrk', query_heads, all_keys, precision=lax.Precision.HIGHEST)
    scores = scores * HEAD_DIM ** (-0.5)
    row_pos = lax.broadcasted_iota(jnp.int32, (ROWS, SUMMARY + ROWS), 0)
    col_pos = lax.broadcasted_iota(jnp.int32, (ROWS, SUMMARY + ROWS), 1)
    scores = jnp.where(col_pos <= row_pos + SUMMARY, scores, jnp.float32(-1e+30))
    row_peak = lax.optimization_barrier(jnp.max(scores, axis=-1, keepdims=True))
    exp_scores = jnp.exp(scores - row_peak)
    return (exp_scores / lax.optimization_barrier(jnp.sum(exp_scores, axis=-1, keepdims=True))).astype(jnp.bfloat16)

def reference(hidden, norm_gain, value_weight, queries, token_keys, summary_keys, output_grad):
    section_hidden = hidden.reshape(TRACE_TOTAL, N_SEG, ROWS, D)
    section_queries = queries.reshape(TRACE_TOTAL, N_SEG, ROWS, HD)
    section_keys = token_keys.reshape(TRACE_TOTAL, N_SEG, ROWS, HD)
    section_summary = summary_keys.reshape(TRACE_TOTAL, N_SEG, SUMMARY, HD)
    section_grad = output_grad.reshape(TRACE_TOTAL, N_SEG, ROWS, HD)
    gain_f = norm_gain.astype(jnp.float32)
    incoming = jnp.zeros((TRACE_TOTAL, SUMMARY, HEADS, HEAD_DIM), jnp.float32)
    weight_grad = jnp.zeros((D, HD), jnp.float32)
    gain_grad = jnp.zeros((D,), jnp.float32)
    hidden_parts = [None] * N_SEG
    summary_parts = [None] * N_SEG
    for section_index in range(N_SEG - 1, -1, -1):
        mixing = mixing_of(section_queries[:, section_index], section_keys[:, section_index], section_summary[:, section_index])
        grad_heads = section_grad[:, section_index].astype(jnp.float32).reshape(TRACE_TOTAL, ROWS, HEADS, HEAD_DIM)
        direct = jnp.einsum('thrk,trhd->tkhd', mixing.astype(jnp.float32), grad_heads, precision=lax.Precision.HIGHEST)
        slot_mixing = mixing[:, :, ROWS - SUMMARY:, :].astype(jnp.float32)
        carried = jnp.einsum('thrk,trhd->tkhd', slot_mixing, incoming, precision=lax.Precision.HIGHEST)
        total = direct + carried
        summary_grad = total[:, :SUMMARY]
        summary_parts[section_index] = summary_grad.reshape(TRACE_TOTAL, SUMMARY, HD)
        value_grad = total[:, SUMMARY:].astype(jnp.bfloat16).reshape(TRACE_TOTAL * ROWS, HD)
        hidden_f = section_hidden[:, section_index].astype(jnp.float32)
        inv_rms = lax.rsqrt(lax.optimization_barrier(jnp.mean(hidden_f * hidden_f, axis=-1, keepdims=True)) + 1e-05)
        normed = hidden_f * inv_rms
        scaled = (normed * gain_f).astype(jnp.bfloat16).reshape(TRACE_TOTAL * ROWS, D)
        weight_grad = weight_grad + lax.dot_general(scaled, value_grad, (((0,), (0,)), ((), ())), preferred_element_type=jnp.float32)
        normalized_gradient = lax.dot_general(value_grad, value_weight, (((1,), (1,)), ((), ())), preferred_element_type=jnp.float32)
        normalized_gradient = normalized_gradient.reshape(TRACE_TOTAL, ROWS, D)
        gain_grad = gain_grad + lax.optimization_barrier(jnp.sum((normalized_gradient * normed).reshape(TRACE_TOTAL * ROWS, D), axis=0))
        scaled_grad = normalized_gradient * gain_f
        hidden_grad = inv_rms * (scaled_grad - normed * lax.optimization_barrier(jnp.mean(scaled_grad * normed, axis=-1, keepdims=True)))
        hidden_parts[section_index] = hidden_grad.astype(jnp.bfloat16)
        incoming = summary_grad
    grad_hidden = jnp.concatenate(hidden_parts, axis=1)
    summary_grads = jnp.concatenate(summary_parts, axis=1)
    return (grad_hidden, summary_grads, weight_grad, gain_grad)
```

```python
import jax
import jax.numpy as jnp
from jax import lax
from jax.sharding import PartitionSpec as P

HEADS = 16
HEAD_DIM = 128


def passed_along(block, axis, distance):
    devices = range(lax.axis_size(axis))
    route = [(i - distance, i) for i in devices if i - distance in devices]
    return lax.ppermute(block, axis, route)


def mixing_of(query_rows, key_rows, summary_rows):
    trace_count, row_count, value_width = query_rows.shape
    slot_count = summary_rows.shape[1]
    query_heads = query_rows.reshape(trace_count, row_count, HEADS, HEAD_DIM)
    all_keys = jnp.concatenate([summary_rows, key_rows], axis=1)
    all_keys = all_keys.reshape(trace_count, slot_count + row_count, HEADS, HEAD_DIM)
    scores = jnp.einsum(
        "trhd,tkhd->thrk", query_heads, all_keys, preferred_element_type=jnp.float32
    )
    scores = scores * HEAD_DIM ** (-0.5)
    row_pos = lax.broadcasted_iota(jnp.int32, (row_count, slot_count + row_count), 0)
    col_pos = lax.broadcasted_iota(jnp.int32, (row_count, slot_count + row_count), 1)
    scores = jnp.where(col_pos <= row_pos + slot_count, scores, jnp.float32(-1e30))
    row_peak = jnp.max(scores, axis=-1, keepdims=True)
    exp_scores = jnp.exp(scores - row_peak)
    return (exp_scores / jnp.sum(exp_scores, axis=-1, keepdims=True)).astype(jnp.bfloat16)


def apply_map(matrix, state):
    return jnp.einsum("thkr,trhd->tkhd", matrix, state, precision=lax.Precision.HIGHEST)


def local(hidden, norm_gain, value_weight, queries, token_keys, summary_keys, output_grad):
    trace_count, row_count, value_width = queries.shape
    slot_count = summary_keys.shape[1]
    model_width = hidden.shape[2]
    mixing = mixing_of(queries, token_keys, summary_keys)
    grad_heads = output_grad.reshape(trace_count, row_count, HEADS, HEAD_DIM)
    direct = jnp.einsum("thrk,trhd->tkhd", mixing, grad_heads, preferred_element_type=jnp.float32)
    slot_mixing = mixing[:, :, row_count - slot_count :, :].astype(jnp.float32)
    own_map = jnp.swapaxes(slot_mixing[..., :slot_count], 2, 3)
    own_offset = direct[:, :slot_count]

    def advance(incoming):
        return apply_map(own_map, incoming) + own_offset

    def one_step(turn_index, incoming):
        outgoing = advance(incoming).reshape(trace_count, slot_count, value_width)
        arrived = passed_along(outgoing, "seg", -1)
        return arrived.reshape(trace_count, slot_count, HEADS, HEAD_DIM)

    start_state = jnp.zeros((trace_count, slot_count, HEADS, HEAD_DIM), jnp.float32)
    incoming = lax.fori_loop(0, lax.axis_size("seg") - 1, one_step, start_state)
    summary_grad = advance(incoming).reshape(trace_count, slot_count, value_width)
    token_part = jnp.einsum(
        "thrk,trhd->tkhd", slot_mixing[..., slot_count:], incoming, precision=lax.Precision.HIGHEST
    )
    value_grad = (direct[:, slot_count:] + token_part).astype(jnp.bfloat16)
    value_grad = value_grad.reshape(trace_count * row_count, value_width)
    hidden_f = hidden.astype(jnp.float32)
    inv_rms = lax.rsqrt(jnp.mean(hidden_f * hidden_f, axis=-1, keepdims=True) + 1e-05)
    normed = hidden_f * inv_rms
    gain_f = norm_gain.astype(jnp.float32)
    scaled = (normed * gain_f).astype(jnp.bfloat16).reshape(trace_count * row_count, model_width)
    weight_grad = lax.dot_general(
        scaled, value_grad, (((0,), (0,)), ((), ())), preferred_element_type=jnp.float32
    )
    normalized_gradient = lax.dot_general(
        value_grad, value_weight, (((1,), (1,)), ((), ())), preferred_element_type=jnp.float32
    )
    normalized_gradient = normalized_gradient.reshape(trace_count, row_count, model_width)
    gain_grad = jnp.sum(
        (normalized_gradient * normed).reshape(trace_count * row_count, model_width), axis=0
    )
    scaled_grad = normalized_gradient * gain_f
    hidden_grad = inv_rms * (
        scaled_grad - normed * jnp.mean(scaled_grad * normed, axis=-1, keepdims=True)
    )
    gain_block = jnp.zeros((model_width, 128), jnp.float32).at[:, 0].set(gain_grad)
    both = jnp.concatenate([weight_grad, gain_block], axis=1)
    both = lax.psum_scatter(both, "seg", scatter_dimension=0, tiled=True)
    both = lax.psum_scatter(both, "dp", scatter_dimension=0, tiled=True)
    weight_part, gain_part = both[:, :value_width], both[:, value_width]
    return (hidden_grad.astype(jnp.bfloat16), summary_grad, weight_part, gain_part)


def solution(mesh):
    placed = (
        P("dp", "seg", None),
        P(),
        P(),
        P("dp", "seg", None),
        P("dp", "seg", None),
        P("dp", "seg", None),
        P("dp", "seg", None),
    )
    return jax.shard_map(
        local,
        mesh=mesh,
        in_specs=placed,
        out_specs=(
            P("dp", "seg", None),
            P("dp", "seg", None),
            P(("seg", "dp"), None),
            P(("seg", "dp")),
        ),
        check_vma=False,
    )
```

```python
import numpy as np
import jax
import jax.numpy as jnp
from jax import lax
from jax.sharding import PartitionSpec as P

HEADS = 16
HEAD_DIM = 128


def passed_along(block, axis, distance):
    devices = range(lax.axis_size(axis))
    route = [(i - distance, i) for i in devices if i - distance in devices]
    return lax.ppermute(block, axis, route)


def mixing_of(query_rows, key_rows, summary_rows):
    trace_count, row_count, value_width = query_rows.shape
    slot_count = summary_rows.shape[1]
    query_heads = query_rows.reshape(trace_count, row_count, HEADS, HEAD_DIM)
    all_keys = jnp.concatenate([summary_rows, key_rows], axis=1)
    all_keys = all_keys.reshape(trace_count, slot_count + row_count, HEADS, HEAD_DIM)
    scores = jnp.einsum(
        "trhd,tkhd->thrk", query_heads, all_keys, preferred_element_type=jnp.float32
    )
    scores = scores * HEAD_DIM ** (-0.5)
    row_pos = lax.broadcasted_iota(jnp.int32, (row_count, slot_count + row_count), 0)
    col_pos = lax.broadcasted_iota(jnp.int32, (row_count, slot_count + row_count), 1)
    scores = jnp.where(col_pos <= row_pos + slot_count, scores, jnp.float32(-1e30))
    row_peak = jnp.max(scores, axis=-1, keepdims=True)
    exp_scores = jnp.exp(scores - row_peak)
    return (exp_scores / jnp.sum(exp_scores, axis=-1, keepdims=True)).astype(jnp.bfloat16)


def apply_map(matrix, state):
    return jnp.einsum("thkr,trhd->tkhd", matrix, state, precision=lax.Precision.HIGHEST)


def ring_step_perm(size, sign):
    return [(i, (i + sign) % size) for i in range(size)]


def ring_reduce(data, coord, axes, forward, backward):
    rows, cols = data.shape
    quarter = data.reshape(4, 2, rows // 8, cols)
    ahead, behind = quarter[:, 0], quarter[:, 1]

    def own(block, index):
        return lax.dynamic_index_in_dim(block, index % 4, 0, keepdims=False)

    acc_a = own(ahead, coord - 1)
    acc_b = own(behind, coord + 1)
    for step in (2, 3, 4):
        acc_a = lax.ppermute(acc_a, axes, forward) + own(ahead, coord - step)
        acc_b = lax.ppermute(acc_b, axes, backward) + own(behind, coord + step)
    return jnp.concatenate([acc_a, acc_b], axis=0)


def shifted(size, move):
    return [(i, move(i)) for i in range(size)]


def reduction_plan(seg_size, dp_size):
    x_n, z_n = seg_size // 4, dp_size // 2

    def coords(s, d):
        return {"x": s // 4, "y": 2 * (d // z_n) + (s // 2) % 2, "z": d % z_n, "core": s % 2}

    def linear(s, d):
        return s * dp_size + d

    def y_move(sign):
        def move(i):
            s, d = divmod(i, dp_size)
            y = (2 * (d // z_n) + (s // 2) % 2 + sign) % 4
            return linear((s // 4) * 4 + (y % 2) * 2 + s % 2, (y // 2) * z_n + d % z_n)
        return move

    perms = {
        "x": [shifted(seg_size, lambda i, g=g: ((i // 4 + g) % x_n) * 4 + i % 4) for g in (1, -1)],
        "z": [shifted(dp_size, lambda i, g=g: (i // z_n) * z_n + (i % z_n + g) % z_n) for g in (1, -1)],
        "y": [shifted(seg_size * dp_size, y_move(g)) for g in (1, -1)],
    }
    axes = {"x": "seg", "z": "dp", "y": ("seg", "dp")}
    return coords, perms, axes


ORDERS = (("x", "y", "z"), ("y", "z", "x"), ("z", "x", "y"))


def row_order(order, seg_size, dp_size, block):
    coords, _, _ = reduction_plan(seg_size, dp_size)
    target = {}
    for s in range(seg_size):
        for d in range(dp_size):
            c = coords(s, d)
            nested = ((c["core"] * 4 + c[order[0]]) * 4 + c[order[1]]) * 4 + c[order[2]]
            target[nested] = s * dp_size + d
    return np.concatenate([np.arange(block) + target[n] * block for n in range(len(target))])


def reduce_scatter_rows(part, order, where):
    coords, perms, axes = reduction_plan(lax.axis_size("seg"), lax.axis_size("dp"))
    rows = part.shape[0]
    core = where["core"]
    half = rows // 2
    send = lax.dynamic_slice_in_dim(part, (1 - core) * half, half, 0)
    keep = lax.dynamic_slice_in_dim(part, core * half, half, 0)
    seg_size = lax.axis_size("seg")
    part = keep + lax.ppermute(send, "seg", shifted(seg_size, lambda i: i ^ 1))
    for dim in order:
        part = ring_reduce(part, where[dim], axes[dim], perms[dim][0], perms[dim][1])
    return part


def local(hidden, norm_gain, value_weight, queries, token_keys, summary_keys, output_grad):
    trace_count, row_count, value_width = queries.shape
    slot_count = summary_keys.shape[1]
    model_width = hidden.shape[2]
    mixing = mixing_of(queries, token_keys, summary_keys)
    grad_heads = output_grad.reshape(trace_count, row_count, HEADS, HEAD_DIM)
    direct = jnp.einsum("thrk,trhd->tkhd", mixing, grad_heads, preferred_element_type=jnp.float32)
    slot_mixing = mixing[:, :, row_count - slot_count :, :].astype(jnp.float32)
    own_map = jnp.swapaxes(slot_mixing[..., :slot_count], 2, 3)
    own_offset = direct[:, :slot_count]

    def advance(incoming):
        return apply_map(own_map, incoming) + own_offset

    def one_step(turn_index, incoming):
        outgoing = advance(incoming).reshape(trace_count, slot_count, value_width)
        arrived = passed_along(outgoing, "seg", -1)
        return arrived.reshape(trace_count, slot_count, HEADS, HEAD_DIM)

    start_state = jnp.zeros((trace_count, slot_count, HEADS, HEAD_DIM), jnp.float32)
    incoming = lax.fori_loop(0, lax.axis_size("seg") - 1, one_step, start_state)
    summary_grad = advance(incoming).reshape(trace_count, slot_count, value_width)
    token_part = jnp.einsum(
        "thrk,trhd->tkhd", slot_mixing[..., slot_count:], incoming, precision=lax.Precision.HIGHEST
    )
    value_grad = (direct[:, slot_count:] + token_part).astype(jnp.bfloat16)
    value_grad = value_grad.reshape(trace_count * row_count, value_width)
    hidden_f = hidden.astype(jnp.float32)
    inv_rms = lax.rsqrt(jnp.mean(hidden_f * hidden_f, axis=-1, keepdims=True) + 1e-05)
    normed = hidden_f * inv_rms
    gain_f = norm_gain.astype(jnp.float32)
    scaled = (normed * gain_f).astype(jnp.bfloat16).reshape(trace_count * row_count, model_width)
    normalized_gradient = lax.dot_general(
        value_grad, value_weight, (((1,), (1,)), ((), ())), preferred_element_type=jnp.float32
    )
    normalized_gradient = normalized_gradient.reshape(trace_count, row_count, model_width)
    gain_grad = jnp.sum(
        (normalized_gradient * normed).reshape(trace_count * row_count, model_width), axis=0
    )
    scaled_grad = normalized_gradient * gain_f
    hidden_grad = inv_rms * (
        scaled_grad - normed * jnp.mean(scaled_grad * normed, axis=-1, keepdims=True)
    )
    seg_index, dp_index = lax.axis_index("seg"), lax.axis_index("dp")
    z_n = lax.axis_size("dp") // 2
    where = {
        "x": seg_index // 4,
        "y": 2 * (dp_index // z_n) + (seg_index // 2) % 2,
        "z": dp_index % z_n,
        "core": seg_index % 2,
    }
    seg_size, dp_size = lax.axis_size("seg"), lax.axis_size("dp")
    block = model_width // (seg_size * dp_size)
    bounds = (0, 768, 1536, value_width)
    pieces = []
    for color, order in enumerate(ORDERS):
        rows = jnp.asarray(row_order(order, seg_size, dp_size, block))
        columns = value_grad[:, bounds[color] : bounds[color + 1]]
        part = lax.dot_general(
            scaled[:, rows], columns, (((0,), (0,)), ((), ())), preferred_element_type=jnp.float32
        )
        if color == len(ORDERS) - 1:
            gain_block = jnp.zeros((model_width, 128), jnp.float32).at[:, 0].set(gain_grad[rows])
            part = jnp.concatenate([part, gain_block], axis=1)
        pieces.append(reduce_scatter_rows(part, order, where))
    both = jnp.concatenate(pieces, axis=1)
    weight_part, gain_part = both[:, :value_width], both[:, value_width]
    return (hidden_grad.astype(jnp.bfloat16), summary_grad, weight_part, gain_part)


def solution(mesh):
    placed = (
        P("dp", "seg", None),
        P(),
        P(),
        P("dp", "seg", None),
        P("dp", "seg", None),
        P("dp", "seg", None),
        P("dp", "seg", None),
    )
    return jax.shard_map(
        local,
        mesh=mesh,
        in_specs=placed,
        out_specs=(
            P("dp", "seg", None),
            P("dp", "seg", None),
            P(("seg", "dp"), None),
            P(("seg", "dp")),
        ),
        check_vma=False,
    )
```

```python
import jax
import jax.numpy as jnp
from jax import lax
from jax.sharding import PartitionSpec as P

HEADS = 16
HEAD_DIM = 128


def passed_along(block, axis, distance):
    devices = range(lax.axis_size(axis))
    route = [(i - distance, i) for i in devices if i - distance in devices]
    return lax.ppermute(block, axis, route)


def mixing_of(query_rows, key_rows, summary_rows):
    trace_count, row_count, value_width = query_rows.shape
    slot_count = summary_rows.shape[1]
    query_heads = query_rows.reshape(trace_count, row_count, HEADS, HEAD_DIM)
    all_keys = jnp.concatenate([summary_rows, key_rows], axis=1)
    all_keys = all_keys.reshape(trace_count, slot_count + row_count, HEADS, HEAD_DIM)
    scores = jnp.einsum(
        "trhd,tkhd->thrk", query_heads, all_keys, preferred_element_type=jnp.float32
    )
    scores = scores * HEAD_DIM ** (-0.5)
    row_pos = lax.broadcasted_iota(jnp.int32, (row_count, slot_count + row_count), 0)
    col_pos = lax.broadcasted_iota(jnp.int32, (row_count, slot_count + row_count), 1)
    scores = jnp.where(col_pos <= row_pos + slot_count, scores, jnp.float32(-1e30))
    row_peak = jnp.max(scores, axis=-1, keepdims=True)
    exp_scores = jnp.exp(scores - row_peak)
    return (exp_scores / jnp.sum(exp_scores, axis=-1, keepdims=True)).astype(jnp.bfloat16)


def apply_map(matrix, state):
    return jnp.einsum("thkr,trhd->tkhd", matrix, state, precision=lax.Precision.HIGHEST)


def shifted(size, move):
    return [(i, move(i)) for i in range(size)]


def reduction_plan(seg_size, dp_size):
    x_n, z_n = seg_size // 4, dp_size // 2

    def y_move(sign):
        def move(i):
            s, d = divmod(i, dp_size)
            y = (2 * (d // z_n) + (s // 2) % 2 + sign) % 4
            return ((s // 4) * 4 + (y % 2) * 2 + s % 2) * dp_size + (y // 2) * z_n + d % z_n
        return move

    perms = {
        "x": [shifted(seg_size, lambda i, g=g: ((i // 4 + g) % x_n) * 4 + i % 4) for g in (1, -1)],
        "z": [shifted(dp_size, lambda i, g=g: (i // z_n) * z_n + (i % z_n + g) % z_n) for g in (1, -1)],
        "y": [shifted(seg_size * dp_size, y_move(g)) for g in (1, -1)],
        "core": shifted(seg_size, lambda i: i ^ 1),
    }
    axes = {"x": "seg", "z": "dp", "y": ("seg", "dp")}
    return perms, axes


ORDERS = (("x", "y", "z"), ("y", "z", "x"), ("z", "x", "y"))


def feature_order(array, order, seg_size, dp_size):
    lead = array.shape[:-1]
    x_n, z_n = seg_size // 4, dp_size // 2
    split = array.reshape(*lead, x_n, 2, 2, 2, z_n, -1)
    n = len(lead)
    place = {"x": [n], "y": [n + 3, n + 1], "z": [n + 4], "core": [n + 2]}
    axes = list(range(n)) + place["core"] + [a for dim in order for a in place[dim]] + [n + 5]
    return split.transpose(axes).reshape(array.shape)


def reduce_colours(parts, where):
    perms, axes = reduction_plan(lax.axis_size("seg"), lax.axis_size("dp"))
    core = where["core"]
    staged = []
    for part in parts:
        half = part.shape[0] // 2
        send = lax.dynamic_slice_in_dim(part, (1 - core) * half, half, 0)
        keep = lax.dynamic_slice_in_dim(part, core * half, half, 0)
        staged.append((keep, lax.ppermute(send, "seg", perms["core"])))
    parts = [keep + got for keep, got in staged]
    for stage in range(3):
        dims = [order[stage] for order in ORDERS]
        split = []
        for part in parts:
            rows, cols = part.shape
            quarter = part.reshape(4, 2, rows // 8, cols)
            split.append((quarter[:, 0], quarter[:, 1]))

        def own(block, index):
            return lax.dynamic_index_in_dim(block, index % 4, 0, keepdims=False)

        acc = [
            [own(ahead, where[dim] - 1), own(behind, where[dim] + 1)]
            for dim, (ahead, behind) in zip(dims, split)
        ]
        for step in (2, 3, 4):
            moved = [
                (
                    lax.ppermute(a, axes[dim], perms[dim][0]),
                    lax.ppermute(b, axes[dim], perms[dim][1]),
                )
                for dim, (a, b) in zip(dims, acc)
            ]
            acc = [
                [a + own(ahead, where[dim] - step), b + own(behind, where[dim] + step)]
                for dim, (a, b), (ahead, behind) in zip(dims, moved, split)
            ]
        parts = [jnp.concatenate(pair, axis=0) for pair in acc]
    return parts


def local(hidden, norm_gain, value_weight, queries, token_keys, summary_keys, output_grad):
    trace_count, row_count, value_width = queries.shape
    slot_count = summary_keys.shape[1]
    model_width = hidden.shape[2]
    mixing = mixing_of(queries, token_keys, summary_keys)
    grad_heads = output_grad.reshape(trace_count, row_count, HEADS, HEAD_DIM)
    direct = jnp.einsum("thrk,trhd->tkhd", mixing, grad_heads, preferred_element_type=jnp.float32)
    slot_mixing = mixing[:, :, row_count - slot_count :, :].astype(jnp.float32)
    own_map = jnp.swapaxes(slot_mixing[..., :slot_count], 2, 3)
    own_offset = direct[:, :slot_count]

    def advance(incoming):
        return apply_map(own_map, incoming) + own_offset

    def one_step(turn_index, incoming):
        outgoing = advance(incoming).reshape(trace_count, slot_count, value_width)
        arrived = passed_along(outgoing, "seg", -1)
        return arrived.reshape(trace_count, slot_count, HEADS, HEAD_DIM)

    start_state = jnp.zeros((trace_count, slot_count, HEADS, HEAD_DIM), jnp.float32)
    incoming = lax.fori_loop(0, lax.axis_size("seg") - 1, one_step, start_state)
    summary_grad = advance(incoming).reshape(trace_count, slot_count, value_width)
    token_part = jnp.einsum(
        "thrk,trhd->tkhd", slot_mixing[..., slot_count:], incoming, precision=lax.Precision.HIGHEST
    )
    value_grad = (direct[:, slot_count:] + token_part).astype(jnp.bfloat16)
    value_grad = value_grad.reshape(trace_count * row_count, value_width)
    hidden_f = hidden.astype(jnp.float32)
    inv_rms = lax.rsqrt(jnp.mean(hidden_f * hidden_f, axis=-1, keepdims=True) + 1e-05)
    normed = hidden_f * inv_rms
    gain_f = norm_gain.astype(jnp.float32)
    scaled = (normed * gain_f).astype(jnp.bfloat16).reshape(trace_count * row_count, model_width)
    normalized_gradient = lax.dot_general(
        value_grad, value_weight, (((1,), (1,)), ((), ())), preferred_element_type=jnp.float32
    )
    normalized_gradient = normalized_gradient.reshape(trace_count, row_count, model_width)
    gain_grad = jnp.sum(
        (normalized_gradient * normed).reshape(trace_count * row_count, model_width), axis=0
    )
    scaled_grad = normalized_gradient * gain_f
    hidden_grad = inv_rms * (
        scaled_grad - normed * jnp.mean(scaled_grad * normed, axis=-1, keepdims=True)
    )
    seg_index, dp_index = lax.axis_index("seg"), lax.axis_index("dp")
    z_n = lax.axis_size("dp") // 2
    where = {
        "x": seg_index // 4,
        "y": 2 * (dp_index // z_n) + (seg_index // 2) % 2,
        "z": dp_index % z_n,
        "core": seg_index % 2,
    }
    seg_size, dp_size = lax.axis_size("seg"), lax.axis_size("dp")
    bounds = (0, 768, 1536, value_width)
    parts = []
    for color, order in enumerate(ORDERS):
        columns = value_grad[:, bounds[color] : bounds[color + 1]]
        part = lax.dot_general(
            feature_order(scaled, order, seg_size, dp_size),
            columns,
            (((0,), (0,)), ((), ())),
            preferred_element_type=jnp.float32,
        )
        if color == len(ORDERS) - 1:
            gain_col = feature_order(gain_grad, order, seg_size, dp_size)
            gain_block = jnp.zeros((model_width, 128), jnp.float32).at[:, 0].set(gain_col)
            part = jnp.concatenate([part, gain_block], axis=1)
        parts.append(part)
    pieces = reduce_colours(parts, where)
    both = jnp.concatenate(pieces, axis=1)
    weight_part, gain_part = both[:, :value_width], both[:, value_width]
    return (hidden_grad.astype(jnp.bfloat16), summary_grad, weight_part, gain_part)


def solution(mesh):
    placed = (
        P("dp", "seg", None),
        P(),
        P(),
        P("dp", "seg", None),
        P("dp", "seg", None),
        P("dp", "seg", None),
        P("dp", "seg", None),
    )
    return jax.shard_map(
        local,
        mesh=mesh,
        in_specs=placed,
        out_specs=(
            P("dp", "seg", None),
            P("dp", "seg", None),
            P(("seg", "dp"), None),
            P(("seg", "dp")),
        ),
        check_vma=False,
    )
```

```python
import jax
import jax.numpy as jnp
from jax import lax
from jax.sharding import PartitionSpec as P

HEADS = 16
HEAD_DIM = 128


def passed_along(block, axis, distance):
    devices = range(lax.axis_size(axis))
    route = [(i - distance, i) for i in devices if i - distance in devices]
    return lax.ppermute(block, axis, route)


def mixing_of(query_rows, key_rows, summary_rows):
    trace_count, row_count, value_width = query_rows.shape
    slot_count = summary_rows.shape[1]
    query_heads = query_rows.reshape(trace_count, row_count, HEADS, HEAD_DIM)
    all_keys = jnp.concatenate([summary_rows, key_rows], axis=1)
    all_keys = all_keys.reshape(trace_count, slot_count + row_count, HEADS, HEAD_DIM)
    scores = jnp.einsum(
        "trhd,tkhd->thrk", query_heads, all_keys, preferred_element_type=jnp.float32
    )
    scores = scores * HEAD_DIM ** (-0.5)
    row_pos = lax.broadcasted_iota(jnp.int32, (row_count, slot_count + row_count), 0)
    col_pos = lax.broadcasted_iota(jnp.int32, (row_count, slot_count + row_count), 1)
    scores = jnp.where(col_pos <= row_pos + slot_count, scores, jnp.float32(-1e30))
    row_peak = jnp.max(scores, axis=-1, keepdims=True)
    exp_scores = jnp.exp(scores - row_peak)
    return (exp_scores / jnp.sum(exp_scores, axis=-1, keepdims=True)).astype(jnp.bfloat16)


def apply_map(matrix, state):
    return jnp.einsum("thkr,trhd->tkhd", matrix, state, precision=lax.Precision.HIGHEST)


def shifted(size, move):
    return [(i, move(i)) for i in range(size)]


def reduction_plan(seg_size, dp_size):
    x_n, z_n = seg_size // 4, dp_size // 2

    def y_move(sign):
        def move(i):
            s, d = divmod(i, dp_size)
            y = (2 * (d // z_n) + (s // 2) % 2 + sign) % 4
            return ((s // 4) * 4 + (y % 2) * 2 + s % 2) * dp_size + (y // 2) * z_n + d % z_n
        return move

    perms = {
        "x": [shifted(seg_size, lambda i, g=g: ((i // 4 + g) % x_n) * 4 + i % 4) for g in (1, -1)],
        "z": [shifted(dp_size, lambda i, g=g: (i // z_n) * z_n + (i % z_n + g) % z_n) for g in (1, -1)],
        "y": [shifted(seg_size * dp_size, y_move(g)) for g in (1, -1)],
        "core": shifted(seg_size, lambda i: i ^ 1),
    }
    axes = {"x": "seg", "z": "dp", "y": ("seg", "dp")}
    return perms, axes


ORDERS = (("x", "y", "z"), ("y", "z", "x"), ("z", "x", "y"))


def feature_order(array, order, seg_size, dp_size):
    lead = array.shape[:-1]
    x_n, z_n = seg_size // 4, dp_size // 2
    split = array.reshape(*lead, x_n, 2, 2, 2, z_n, -1)
    n = len(lead)
    place = {"x": [n], "y": [n + 3, n + 1], "z": [n + 4], "core": [n + 2]}
    axes = list(range(n)) + place["core"] + [a for dim in order for a in place[dim]] + [n + 5]
    return split.transpose(axes).reshape(array.shape)


def reduce_colours(parts, where):
    perms, axes = reduction_plan(lax.axis_size("seg"), lax.axis_size("dp"))
    core = where["core"]
    staged = []
    for part in parts:
        half = part.shape[0] // 2
        send = lax.dynamic_slice_in_dim(part, (1 - core) * half, half, 0)
        keep = lax.dynamic_slice_in_dim(part, core * half, half, 0)
        staged.append((keep, lax.ppermute(send, "seg", perms["core"])))
    parts = [keep + got for keep, got in staged]
    for stage in range(3):
        dims = [order[stage] for order in ORDERS]
        split = []
        for part in parts:
            rows, cols = part.shape
            quarter = part.reshape(4, 2, rows // 8, cols)
            split.append((quarter[:, 0], quarter[:, 1]))

        def own(block, index):
            return lax.dynamic_index_in_dim(block, index % 4, 0, keepdims=False)

        acc = [
            [own(ahead, where[dim] - 1), own(behind, where[dim] + 1)]
            for dim, (ahead, behind) in zip(dims, split)
        ]
        for step in (2, 3, 4):
            moved = [
                (
                    lax.ppermute(a, axes[dim], perms[dim][0]),
                    lax.ppermute(b, axes[dim], perms[dim][1]),
                )
                for dim, (a, b) in zip(dims, acc)
            ]
            acc = [
                [a + own(ahead, where[dim] - step), b + own(behind, where[dim] + step)]
                for dim, (a, b), (ahead, behind) in zip(dims, moved, split)
            ]
        parts = [jnp.concatenate(pair, axis=0) for pair in acc]
    return parts


def local(hidden, norm_gain, value_weight, queries, token_keys, summary_keys, output_grad):
    trace_count, row_count, value_width = queries.shape
    slot_count = summary_keys.shape[1]
    model_width = hidden.shape[2]
    mixing = mixing_of(queries, token_keys, summary_keys)
    grad_heads = output_grad.reshape(trace_count, row_count, HEADS, HEAD_DIM)
    direct = jnp.einsum("thrk,trhd->tkhd", mixing, grad_heads, preferred_element_type=jnp.float32)
    slot_mixing = mixing[:, :, row_count - slot_count :, :].astype(jnp.float32)
    own_map = jnp.swapaxes(slot_mixing[..., :slot_count], 2, 3)
    own_offset = direct[:, :slot_count]

    chain_map, chain_offset = own_map, own_offset
    offset, seg_size = 1, lax.axis_size("seg")
    while offset < seg_size:
        last = 2 * offset >= seg_size
        far_offset = passed_along(chain_offset, "seg", -offset)
        new_offset = apply_map(chain_map, far_offset) + chain_offset
        if not last:
            far_map = passed_along(chain_map, "seg", -offset)
            chain_map = jnp.einsum(
                "thkm,thmr->thkr", chain_map, far_map, precision=lax.Precision.HIGHEST
            )
        chain_offset = new_offset
        offset *= 2
    summary_grad = chain_offset.reshape(trace_count, slot_count, value_width)
    incoming = passed_along(summary_grad, "seg", -1).reshape(chain_offset.shape)
    token_part = jnp.einsum(
        "thrk,trhd->tkhd", slot_mixing[..., slot_count:], incoming, precision=lax.Precision.HIGHEST
    )
    value_grad = (direct[:, slot_count:] + token_part).astype(jnp.bfloat16)
    value_grad = value_grad.reshape(trace_count * row_count, value_width)
    hidden_f = hidden.astype(jnp.float32)
    inv_rms = lax.rsqrt(jnp.mean(hidden_f * hidden_f, axis=-1, keepdims=True) + 1e-05)
    normed = hidden_f * inv_rms
    gain_f = norm_gain.astype(jnp.float32)
    scaled = (normed * gain_f).astype(jnp.bfloat16).reshape(trace_count * row_count, model_width)
    normalized_gradient = lax.dot_general(
        value_grad, value_weight, (((1,), (1,)), ((), ())), preferred_element_type=jnp.float32
    )
    normalized_gradient = normalized_gradient.reshape(trace_count, row_count, model_width)
    gain_grad = jnp.sum(
        (normalized_gradient * normed).reshape(trace_count * row_count, model_width), axis=0
    )
    scaled_grad = normalized_gradient * gain_f
    hidden_grad = inv_rms * (
        scaled_grad - normed * jnp.mean(scaled_grad * normed, axis=-1, keepdims=True)
    )
    seg_index, dp_index = lax.axis_index("seg"), lax.axis_index("dp")
    z_n = lax.axis_size("dp") // 2
    where = {
        "x": seg_index // 4,
        "y": 2 * (dp_index // z_n) + (seg_index // 2) % 2,
        "z": dp_index % z_n,
        "core": seg_index % 2,
    }
    seg_size, dp_size = lax.axis_size("seg"), lax.axis_size("dp")
    bounds = (0, 768, 1536, value_width)
    parts = []
    for color, order in enumerate(ORDERS):
        columns = value_grad[:, bounds[color] : bounds[color + 1]]
        part = lax.dot_general(
            feature_order(scaled, order, seg_size, dp_size),
            columns,
            (((0,), (0,)), ((), ())),
            preferred_element_type=jnp.float32,
        )
        if color == len(ORDERS) - 1:
            gain_col = feature_order(gain_grad, order, seg_size, dp_size)
            gain_block = jnp.zeros((model_width, 128), jnp.float32).at[:, 0].set(gain_col)
            part = jnp.concatenate([part, gain_block], axis=1)
        parts.append(part)
    pieces = reduce_colours(parts, where)
    both = jnp.concatenate(pieces, axis=1)
    weight_part, gain_part = both[:, :value_width], both[:, value_width]
    return (hidden_grad.astype(jnp.bfloat16), summary_grad, weight_part, gain_part)


def solution(mesh):
    placed = (
        P("dp", "seg", None),
        P(),
        P(),
        P("dp", "seg", None),
        P("dp", "seg", None),
        P("dp", "seg", None),
        P("dp", "seg", None),
    )
    return jax.shard_map(
        local,
        mesh=mesh,
        in_specs=placed,
        out_specs=(
            P("dp", "seg", None),
            P("dp", "seg", None),
            P(("seg", "dp"), None),
            P(("seg", "dp")),
        ),
        check_vma=False,
    )
```

```python
import jax
import jax.numpy as jnp
from jax import lax
from jax.sharding import PartitionSpec as P

HEADS = 16
HEAD_DIM = 128


def passed_along(block, axis, distance):
    devices = range(lax.axis_size(axis))
    route = [(i - distance, i) for i in devices if i - distance in devices]
    return lax.ppermute(block, axis, route)


def mixing_of(query_rows, key_rows, summary_rows):
    trace_count, row_count, value_width = query_rows.shape
    slot_count = summary_rows.shape[1]
    query_heads = query_rows.reshape(trace_count, row_count, HEADS, HEAD_DIM)
    all_keys = jnp.concatenate([summary_rows, key_rows], axis=1)
    all_keys = all_keys.reshape(trace_count, slot_count + row_count, HEADS, HEAD_DIM)
    scores = jnp.einsum(
        "trhd,tkhd->thrk", query_heads, all_keys, preferred_element_type=jnp.float32
    )
    scores = scores * HEAD_DIM ** (-0.5)
    row_pos = lax.broadcasted_iota(jnp.int32, (row_count, slot_count + row_count), 0)
    col_pos = lax.broadcasted_iota(jnp.int32, (row_count, slot_count + row_count), 1)
    scores = jnp.where(col_pos <= row_pos + slot_count, scores, jnp.float32(-1e30))
    row_peak = jnp.max(scores, axis=-1, keepdims=True)
    exp_scores = jnp.exp(scores - row_peak)
    return (exp_scores / jnp.sum(exp_scores, axis=-1, keepdims=True)).astype(jnp.bfloat16)


def apply_map(matrix, state):
    return jnp.einsum("thkr,trhd->tkhd", matrix, state, precision=lax.Precision.HIGHEST)


def shifted(size, move):
    return [(i, move(i)) for i in range(size)]


def reduction_plan(seg_size, dp_size):
    x_n, z_n = seg_size // 4, dp_size // 2

    def y_move(sign):
        def move(i):
            s, d = divmod(i, dp_size)
            y = (2 * (d // z_n) + (s // 2) % 2 + sign) % 4
            return ((s // 4) * 4 + (y % 2) * 2 + s % 2) * dp_size + (y // 2) * z_n + d % z_n
        return move

    perms = {
        "x": [shifted(seg_size, lambda i, g=g: ((i // 4 + g) % x_n) * 4 + i % 4) for g in (1, -1, 2)],
        "z": [shifted(dp_size, lambda i, g=g: (i // z_n) * z_n + (i % z_n + g) % z_n) for g in (1, -1, 2)],
        "y": [shifted(seg_size * dp_size, y_move(g)) for g in (1, -1, 2)],
        "core": shifted(seg_size, lambda i: i ^ 1),
    }
    axes = {"x": "seg", "z": "dp", "y": ("seg", "dp")}
    return perms, axes


ORDERS = (("x", "y", "z"), ("y", "z", "x"), ("z", "x", "y"))


def feature_order(array, order, seg_size, dp_size):
    lead = array.shape[:-1]
    x_n, z_n = seg_size // 4, dp_size // 2
    split = array.reshape(*lead, x_n, 2, 2, 2, z_n, -1)
    n = len(lead)
    place = {"x": [n], "y": [n + 3, n + 1], "z": [n + 4], "core": [n + 2]}
    axes = list(range(n)) + place["core"] + [a for dim in order for a in place[dim]] + [n + 5]
    return split.transpose(axes).reshape(array.shape)


def reduce_colours(halves, where):
    perms, axes = reduction_plan(lax.axis_size("seg"), lax.axis_size("dp"))
    parts = [keep + lax.ppermute(send, "seg", perms["core"]) for keep, send in halves]
    for stage in range(3):
        dims = [order[stage] for order in ORDERS]
        moved = []
        for dim, part in zip(dims, parts):
            rows, cols = part.shape
            chunks = part.reshape(4, rows // 4, cols)

            def own(index, chunks=chunks):
                return lax.dynamic_index_in_dim(chunks, index % 4, 0, keepdims=False)

            coord = where[dim]
            sends = [
                lax.ppermute(own(coord + 1), axes[dim], perms[dim][0]),
                lax.ppermute(own(coord - 1), axes[dim], perms[dim][1]),
                lax.ppermute(own(coord + 2), axes[dim], perms[dim][2]),
            ]
            moved.append((own(coord), sends))
        parts = [mine + sends[0] + sends[1] + sends[2] for mine, sends in moved]
    return parts


def local(hidden, norm_gain, value_weight, queries, token_keys, summary_keys, output_grad):
    trace_count, row_count, value_width = queries.shape
    slot_count = summary_keys.shape[1]
    model_width = hidden.shape[2]
    mixing = mixing_of(queries, token_keys, summary_keys)
    grad_heads = output_grad.reshape(trace_count, row_count, HEADS, HEAD_DIM)
    direct = jnp.einsum("thrk,trhd->tkhd", mixing, grad_heads, preferred_element_type=jnp.float32)
    slot_mixing = mixing[:, :, row_count - slot_count :, :].astype(jnp.float32)
    own_map = jnp.swapaxes(slot_mixing[..., :slot_count], 2, 3)
    own_offset = direct[:, :slot_count]

    chain_map, chain_offset = own_map, own_offset
    offset, seg_size = 1, lax.axis_size("seg")
    while offset < seg_size:
        last = 2 * offset >= seg_size
        far_offset = passed_along(chain_offset, "seg", -offset)
        new_offset = apply_map(chain_map, far_offset) + chain_offset
        if not last:
            far_map = passed_along(chain_map, "seg", -offset)
            chain_map = jnp.einsum(
                "thkm,thmr->thkr", chain_map, far_map, precision=lax.Precision.HIGHEST
            )
        chain_offset = new_offset
        offset *= 2
    summary_grad = chain_offset.reshape(trace_count, slot_count, value_width)
    incoming = passed_along(summary_grad, "seg", -1).reshape(chain_offset.shape)
    token_part = jnp.einsum(
        "thrk,trhd->tkhd", slot_mixing[..., slot_count:], incoming, precision=lax.Precision.HIGHEST
    )
    value_grad = (direct[:, slot_count:] + token_part).astype(jnp.bfloat16)
    value_grad = value_grad.reshape(trace_count * row_count, value_width)
    hidden_f = hidden.astype(jnp.float32)
    inv_rms = lax.rsqrt(jnp.mean(hidden_f * hidden_f, axis=-1, keepdims=True) + 1e-05)
    normed = hidden_f * inv_rms
    gain_f = norm_gain.astype(jnp.float32)
    scaled = (normed * gain_f).astype(jnp.bfloat16).reshape(trace_count * row_count, model_width)
    normalized_gradient = lax.dot_general(
        value_grad, value_weight, (((1,), (1,)), ((), ())), preferred_element_type=jnp.float32
    )
    normalized_gradient = normalized_gradient.reshape(trace_count, row_count, model_width)
    gain_grad = jnp.sum(
        (normalized_gradient * normed).reshape(trace_count * row_count, model_width), axis=0
    )
    scaled_grad = normalized_gradient * gain_f
    hidden_grad = inv_rms * (
        scaled_grad - normed * jnp.mean(scaled_grad * normed, axis=-1, keepdims=True)
    )
    seg_index, dp_index = lax.axis_index("seg"), lax.axis_index("dp")
    z_n = lax.axis_size("dp") // 2
    where = {
        "x": seg_index // 4,
        "y": 2 * (dp_index // z_n) + (seg_index // 2) % 2,
        "z": dp_index % z_n,
        "core": seg_index % 2,
    }
    seg_size, dp_size = lax.axis_size("seg"), lax.axis_size("dp")
    bounds = (0, 768, 1536, value_width)
    halves = []
    half = model_width // 2
    core = where["core"]
    for color, order in enumerate(ORDERS):
        columns = value_grad[:, bounds[color] : bounds[color + 1]]
        ordered = feature_order(scaled, order, seg_size, dp_size)
        pair = []
        for pick in (core, 1 - core):
            rows = lax.dynamic_slice_in_dim(ordered, pick * half, half, 1)
            part = lax.dot_general(
                rows, columns, (((0,), (0,)), ((), ())), preferred_element_type=jnp.float32
            )
            if color == len(ORDERS) - 1:
                gain_col = feature_order(gain_grad, order, seg_size, dp_size)
                gain_col = lax.dynamic_slice_in_dim(gain_col, pick * half, half, 0)
                gain_block = jnp.zeros((half, 128), jnp.float32).at[:, 0].set(gain_col)
                part = jnp.concatenate([part, gain_block], axis=1)
            pair.append(part)
        halves.append(pair)
    pieces = reduce_colours(halves, where)
    both = jnp.concatenate(pieces, axis=1)
    weight_part, gain_part = both[:, :value_width], both[:, value_width]
    return (hidden_grad.astype(jnp.bfloat16), summary_grad, weight_part, gain_part)


def solution(mesh):
    placed = (
        P("dp", "seg", None),
        P(),
        P(),
        P("dp", "seg", None),
        P("dp", "seg", None),
        P("dp", "seg", None),
        P("dp", "seg", None),
    )
    return jax.shard_map(
        local,
        mesh=mesh,
        in_specs=placed,
        out_specs=(
            P("dp", "seg", None),
            P("dp", "seg", None),
            P(("seg", "dp"), None),
            P(("seg", "dp")),
        ),
        check_vma=False,
    )
```

```python
import jax
import jax.numpy as jnp
from jax import lax
from jax.sharding import PartitionSpec as P

HEADS = 16
HEAD_DIM = 128


def passed_along(block, axis, distance):
    devices = range(lax.axis_size(axis))
    route = [(i - distance, i) for i in devices if i - distance in devices]
    return lax.ppermute(block, axis, route)


def mixing_of(query_rows, key_rows, summary_rows):
    trace_count, row_count, value_width = query_rows.shape
    slot_count = summary_rows.shape[1]
    query_heads = query_rows.reshape(trace_count, row_count, HEADS, HEAD_DIM)
    all_keys = jnp.concatenate([summary_rows, key_rows], axis=1)
    all_keys = all_keys.reshape(trace_count, slot_count + row_count, HEADS, HEAD_DIM)
    scores = jnp.einsum(
        "trhd,tkhd->thrk", query_heads, all_keys, preferred_element_type=jnp.float32
    )
    scores = scores * HEAD_DIM ** (-0.5)
    row_pos = lax.broadcasted_iota(jnp.int32, (row_count, slot_count + row_count), 0)
    col_pos = lax.broadcasted_iota(jnp.int32, (row_count, slot_count + row_count), 1)
    scores = jnp.where(col_pos <= row_pos + slot_count, scores, jnp.float32(-1e30))
    row_peak = jnp.max(scores, axis=-1, keepdims=True)
    exp_scores = jnp.exp(scores - row_peak)
    return (exp_scores / jnp.sum(exp_scores, axis=-1, keepdims=True)).astype(jnp.bfloat16)


def apply_map(matrix, state):
    return jnp.einsum("thkr,trhd->tkhd", matrix, state, precision=lax.Precision.HIGHEST)


def shifted(size, move):
    return [(i, move(i)) for i in range(size)]


def reduction_plan(seg_size, dp_size):
    x_n, z_n = seg_size // 4, dp_size // 2

    def y_move(sign):
        def move(i):
            s, d = divmod(i, dp_size)
            y = (2 * (d // z_n) + (s // 2) % 2 + sign) % 4
            return ((s // 4) * 4 + (y % 2) * 2 + s % 2) * dp_size + (y // 2) * z_n + d % z_n
        return move

    perms = {
        "x": [shifted(seg_size, lambda i, g=g: ((i // 4 + g) % x_n) * 4 + i % 4) for g in (1, -1, 2)],
        "z": [shifted(dp_size, lambda i, g=g: (i // z_n) * z_n + (i % z_n + g) % z_n) for g in (1, -1, 2)],
        "y": [shifted(seg_size * dp_size, y_move(g)) for g in (1, -1, 2)],
        "core": shifted(seg_size, lambda i: i ^ 1),
    }
    axes = {"x": "seg", "z": "dp", "y": ("seg", "dp")}
    return perms, axes


ORDERS = (("x", "y", "z"), ("y", "z", "x"), ("z", "x", "y"))


def feature_order(array, order, seg_size, dp_size):
    lead = array.shape[:-1]
    x_n, z_n = seg_size // 4, dp_size // 2
    split = array.reshape(*lead, x_n, 2, 2, 2, z_n, -1)
    n = len(lead)
    place = {"x": [n], "y": [n + 3, n + 1], "z": [n + 4], "core": [n + 2]}
    axes = list(range(n)) + place["core"] + [a for dim in order for a in place[dim]] + [n + 5]
    return split.transpose(axes).reshape(array.shape)


def reduce_colours(halves, where):
    perms, axes = reduction_plan(lax.axis_size("seg"), lax.axis_size("dp"))
    parts = [keep + lax.ppermute(send, "seg", perms["core"]) for keep, send in halves]
    for stage in range(3):
        dims = [order[stage] for order in ORDERS]
        moved = []
        for dim, part in zip(dims, parts):
            rows, cols = part.shape
            chunks = part.reshape(4, rows // 4, cols)

            def own(index, chunks=chunks):
                return lax.dynamic_index_in_dim(chunks, index % 4, 0, keepdims=False)

            coord = where[dim]
            sends = [
                lax.ppermute(own(coord + 1), axes[dim], perms[dim][0]),
                lax.ppermute(own(coord - 1), axes[dim], perms[dim][1]),
                lax.ppermute(own(coord + 2), axes[dim], perms[dim][2]),
            ]
            moved.append((own(coord), sends))
        parts = [mine + sends[0] + sends[1] + sends[2] for mine, sends in moved]
    return parts


def local(hidden, norm_gain, value_weight, queries, token_keys, summary_keys, output_grad):
    trace_count, row_count, value_width = queries.shape
    slot_count = summary_keys.shape[1]
    model_width = hidden.shape[2]
    mixing = mixing_of(queries, token_keys, summary_keys)
    grad_heads = output_grad.reshape(trace_count, row_count, HEADS, HEAD_DIM)
    direct = jnp.einsum("thrk,trhd->tkhd", mixing, grad_heads, preferred_element_type=jnp.float32)
    slot_mixing = mixing[:, :, row_count - slot_count :, :].astype(jnp.float32)
    own_map = jnp.swapaxes(slot_mixing[..., :slot_count], 2, 3)
    own_offset = direct[:, :slot_count]

    chain_map, chain_offset = own_map, own_offset
    offset, seg_size = 1, lax.axis_size("seg")
    while offset < seg_size:
        last = 2 * offset >= seg_size
        far_offset = passed_along(chain_offset, "seg", -offset)
        new_offset = apply_map(chain_map, far_offset) + chain_offset
        if not last:
            far_map = passed_along(chain_map, "seg", -offset)
            chain_map = jnp.einsum(
                "thkm,thmr->thkr", chain_map, far_map, precision=lax.Precision.HIGHEST
            )
        chain_offset = new_offset
        offset *= 2
    summary_grad = chain_offset.reshape(trace_count, slot_count, value_width)
    incoming = passed_along(summary_grad, "seg", -1).reshape(chain_offset.shape)
    token_part = jnp.einsum(
        "thrk,trhd->tkhd", slot_mixing[..., slot_count:], incoming, precision=lax.Precision.HIGHEST
    )
    value_grad = (direct[:, slot_count:] + token_part).astype(jnp.bfloat16)
    value_grad = value_grad.reshape(trace_count * row_count, value_width)
    hidden_f = hidden.astype(jnp.float32)
    inv_rms = lax.rsqrt(jnp.mean(hidden_f * hidden_f, axis=-1, keepdims=True) + 1e-05)
    normed = hidden_f * inv_rms
    gain_f = norm_gain.astype(jnp.float32)
    scaled = (normed * gain_f).astype(jnp.bfloat16).reshape(trace_count * row_count, model_width)
    normalized_gradient = lax.dot_general(
        value_grad, value_weight, (((1,), (1,)), ((), ())), preferred_element_type=jnp.float32
    )
    normalized_gradient = normalized_gradient.reshape(trace_count, row_count, model_width)
    gain_grad = jnp.sum(
        (normalized_gradient * normed).reshape(trace_count * row_count, model_width), axis=0
    )
    scaled_grad = normalized_gradient * gain_f
    hidden_grad = inv_rms * (
        scaled_grad - normed * jnp.mean(scaled_grad * normed, axis=-1, keepdims=True)
    )
    seg_index, dp_index = lax.axis_index("seg"), lax.axis_index("dp")
    z_n = lax.axis_size("dp") // 2
    where = {
        "x": seg_index // 4,
        "y": 2 * (dp_index // z_n) + (seg_index // 2) % 2,
        "z": dp_index % z_n,
        "core": seg_index % 2,
    }
    seg_size, dp_size = lax.axis_size("seg"), lax.axis_size("dp")
    bounds = (0, 768, 1536, value_width)
    halves = []
    half = model_width // 2
    core = where["core"]
    for color, order in enumerate(ORDERS):
        columns = value_grad[:, bounds[color] : bounds[color + 1]]
        last = color == len(ORDERS) - 1
        if last:
            spare = jnp.zeros((columns.shape[0], 128), columns.dtype)
            columns = jnp.concatenate([columns, spare], axis=1)
            gain_col = feature_order(gain_grad, order, seg_size, dp_size)
        ordered = feature_order(scaled, order, seg_size, dp_size)
        pair = []
        for pick in (core, 1 - core):
            rows = lax.dynamic_slice_in_dim(ordered, pick * half, half, 1)
            part = lax.dot_general(
                rows, columns, (((0,), (0,)), ((), ())), preferred_element_type=jnp.float32
            )
            if last:
                lane = lax.broadcasted_iota(jnp.int32, part.shape, 1)
                gain_half = lax.dynamic_slice_in_dim(gain_col, pick * half, half, 0)
                gain_lane = part.shape[1] - 128
                part = part + jnp.where(lane == gain_lane, gain_half[:, None], jnp.float32(0))
            pair.append(part)
        halves.append(pair)
    pieces = reduce_colours(halves, where)
    both = jnp.concatenate(pieces, axis=1)
    weight_part, gain_part = both[:, :value_width], both[:, value_width]
    return (hidden_grad.astype(jnp.bfloat16), summary_grad, weight_part, gain_part)


def solution(mesh):
    placed = (
        P("dp", "seg", None),
        P(),
        P(),
        P("dp", "seg", None),
        P("dp", "seg", None),
        P("dp", "seg", None),
        P("dp", "seg", None),
    )
    return jax.shard_map(
        local,
        mesh=mesh,
        in_specs=placed,
        out_specs=(
            P("dp", "seg", None),
            P("dp", "seg", None),
            P(("seg", "dp"), None),
            P(("seg", "dp")),
        ),
        check_vma=False,
    )
```

```python
import jax
import jax.numpy as jnp
from jax import lax
from jax.sharding import PartitionSpec as P

HEADS = 16
HEAD_DIM = 128


def passed_along(block, axis, distance):
    devices = range(lax.axis_size(axis))
    route = [(i - distance, i) for i in devices if i - distance in devices]
    return lax.ppermute(block, axis, route)


def mixing_of(query_rows, key_rows, summary_rows):
    trace_count, row_count, value_width = query_rows.shape
    slot_count = summary_rows.shape[1]
    query_heads = query_rows.reshape(trace_count, row_count, HEADS, HEAD_DIM)
    all_keys = jnp.concatenate([summary_rows, key_rows], axis=1)
    all_keys = all_keys.reshape(trace_count, slot_count + row_count, HEADS, HEAD_DIM)
    scores = jnp.einsum(
        "trhd,tkhd->thrk", query_heads, all_keys, preferred_element_type=jnp.float32
    )
    scores = scores * HEAD_DIM ** (-0.5)
    row_pos = lax.broadcasted_iota(jnp.int32, (row_count, slot_count + row_count), 0)
    col_pos = lax.broadcasted_iota(jnp.int32, (row_count, slot_count + row_count), 1)
    scores = jnp.where(col_pos <= row_pos + slot_count, scores, jnp.float32(-1e30))
    row_peak = jnp.max(scores, axis=-1, keepdims=True)
    exp_scores = jnp.exp(scores - row_peak)
    return (exp_scores / jnp.sum(exp_scores, axis=-1, keepdims=True)).astype(jnp.bfloat16)


def apply_map(matrix, state):
    return jnp.einsum("thkr,trhd->tkhd", matrix, state, precision=lax.Precision.HIGHEST)


def shifted(size, move):
    return [(i, move(i)) for i in range(size)]


def reduction_plan(seg_size, dp_size):
    x_n, z_n = seg_size // 4, dp_size // 2

    def y_move(sign):
        def move(i):
            s, d = divmod(i, dp_size)
            y = (2 * (d // z_n) + (s // 2) % 2 + sign) % 4
            return ((s // 4) * 4 + (y % 2) * 2 + s % 2) * dp_size + (y // 2) * z_n + d % z_n
        return move

    perms = {
        "x": [shifted(seg_size, lambda i, g=g: ((i // 4 + g) % x_n) * 4 + i % 4) for g in (1, -1, 2)],
        "z": [shifted(dp_size, lambda i, g=g: (i // z_n) * z_n + (i % z_n + g) % z_n) for g in (1, -1, 2)],
        "y": [shifted(seg_size * dp_size, y_move(g)) for g in (1, -1, 2)],
        "core": shifted(seg_size, lambda i: i ^ 1),
    }
    axes = {"x": "seg", "z": "dp", "y": ("seg", "dp")}
    return perms, axes


ORDERS = (("x", "y", "z"), ("y", "z", "x"), ("z", "x", "y"))


def feature_order(array, order, seg_size, dp_size):
    lead = array.shape[:-1]
    x_n, z_n = seg_size // 4, dp_size // 2
    split = array.reshape(*lead, x_n, 2, 2, 2, z_n, -1)
    n = len(lead)
    place = {"x": [n], "y": [n + 3, n + 1], "z": [n + 4], "core": [n + 2]}
    axes = list(range(n)) + place["core"] + [a for dim in order for a in place[dim]] + [n + 5]
    return split.transpose(axes).reshape(array.shape)


def reduce_colours(halves, where):
    perms, axes = reduction_plan(lax.axis_size("seg"), lax.axis_size("dp"))
    parts = [keep + lax.ppermute(send, "seg", perms["core"]) for keep, send in halves]
    return ring_stages(parts, where, perms, axes)


def ring_stages(parts, where, perms, axes):
    for stage in range(3):
        dims = [order[stage] for order in ORDERS]
        moved = []
        for dim, part in zip(dims, parts):
            rows, cols = part.shape
            chunks = part.reshape(4, rows // 4, cols)

            def own(index, chunks=chunks):
                return lax.dynamic_index_in_dim(chunks, index % 4, 0, keepdims=False)

            coord = where[dim]
            sends = [
                lax.ppermute(own(coord + 1), axes[dim], perms[dim][0]),
                lax.ppermute(own(coord - 1), axes[dim], perms[dim][1]),
                lax.ppermute(own(coord + 2), axes[dim], perms[dim][2]),
            ]
            moved.append((own(coord), sends))
        parts = [mine + sends[0] + sends[1] + sends[2] for mine, sends in moved]
    return parts


def local(hidden, norm_gain, value_weight, queries, token_keys, summary_keys, output_grad):
    trace_count, row_count, value_width = queries.shape
    slot_count = summary_keys.shape[1]
    model_width = hidden.shape[2]
    mixing = mixing_of(queries, token_keys, summary_keys)
    grad_heads = output_grad.reshape(trace_count, row_count, HEADS, HEAD_DIM)
    direct = jnp.einsum("thrk,trhd->tkhd", mixing, grad_heads, preferred_element_type=jnp.float32)
    slot_mixing = mixing[:, :, row_count - slot_count :, :].astype(jnp.float32)
    own_map = jnp.swapaxes(slot_mixing[..., :slot_count], 2, 3)
    own_offset = direct[:, :slot_count]

    chain_map, chain_offset = own_map, own_offset
    offset, seg_size = 1, lax.axis_size("seg")
    while offset < seg_size:
        last = 2 * offset >= seg_size
        if last:
            far_offset = passed_along(chain_offset, "seg", -offset)
        else:
            packed = jnp.concatenate([chain_offset.reshape(-1), chain_map.reshape(-1)])
            far = passed_along(packed, "seg", -offset)
            far_offset = far[: chain_offset.size].reshape(chain_offset.shape)
            far_map = far[chain_offset.size :].reshape(chain_map.shape)
        new_offset = apply_map(chain_map, far_offset) + chain_offset
        if not last:
            chain_map = jnp.einsum(
                "thkm,thmr->thkr", chain_map, far_map, precision=lax.Precision.HIGHEST
            )
        chain_offset = new_offset
        offset *= 2
    summary_grad = chain_offset.reshape(trace_count, slot_count, value_width)
    incoming = passed_along(summary_grad, "seg", -1).reshape(chain_offset.shape)
    token_part = jnp.einsum(
        "thrk,trhd->tkhd", slot_mixing[..., slot_count:], incoming, precision=lax.Precision.HIGHEST
    )
    value_grad = (direct[:, slot_count:] + token_part).astype(jnp.bfloat16)
    value_grad = value_grad.reshape(trace_count * row_count, value_width)
    hidden_f = hidden.astype(jnp.float32)
    inv_rms = lax.rsqrt(jnp.mean(hidden_f * hidden_f, axis=-1, keepdims=True) + 1e-05)
    normed = hidden_f * inv_rms
    gain_f = norm_gain.astype(jnp.float32)
    scaled = (normed * gain_f).astype(jnp.bfloat16).reshape(trace_count * row_count, model_width)
    normalized_gradient = lax.dot_general(
        value_grad, value_weight, (((1,), (1,)), ((), ())), preferred_element_type=jnp.float32
    )
    normalized_gradient = normalized_gradient.reshape(trace_count, row_count, model_width)
    gain_grad = jnp.sum(
        (normalized_gradient * normed).reshape(trace_count * row_count, model_width), axis=0
    )
    scaled_grad = normalized_gradient * gain_f
    hidden_grad = inv_rms * (
        scaled_grad - normed * jnp.mean(scaled_grad * normed, axis=-1, keepdims=True)
    )
    seg_index, dp_index = lax.axis_index("seg"), lax.axis_index("dp")
    z_n = lax.axis_size("dp") // 2
    where = {
        "x": seg_index // 4,
        "y": 2 * (dp_index // z_n) + (seg_index // 2) % 2,
        "z": dp_index % z_n,
        "core": seg_index % 2,
    }
    seg_size, dp_size = lax.axis_size("seg"), lax.axis_size("dp")
    bounds = (0, 768, 1536, value_width)
    halves = []
    half = model_width // 2
    core = where["core"]
    for color, order in enumerate(ORDERS):
        columns = value_grad[:, bounds[color] : bounds[color + 1]]
        last = color == len(ORDERS) - 1
        if last:
            spare = jnp.zeros((columns.shape[0], 128), columns.dtype)
            columns = jnp.concatenate([columns, spare], axis=1)
            gain_col = feature_order(gain_grad, order, seg_size, dp_size)
        ordered = feature_order(scaled, order, seg_size, dp_size)
        pair = []
        for pick in (core, 1 - core):
            rows = lax.dynamic_slice_in_dim(ordered, pick * half, half, 1)
            part = lax.dot_general(
                rows, columns, (((0,), (0,)), ((), ())), preferred_element_type=jnp.float32
            )
            if last:
                lane = lax.broadcasted_iota(jnp.int32, part.shape, 1)
                gain_half = lax.dynamic_slice_in_dim(gain_col, pick * half, half, 0)
                gain_lane = part.shape[1] - 128
                part = part + jnp.where(lane == gain_lane, gain_half[:, None], jnp.float32(0))
            pair.append(part)
        halves.append(pair)
    pieces = reduce_colours(halves, where)
    both = jnp.concatenate(pieces, axis=1)
    weight_part, gain_part = both[:, :value_width], both[:, value_width]
    return (hidden_grad.astype(jnp.bfloat16), summary_grad, weight_part, gain_part)


def solution(mesh):
    placed = (
        P("dp", "seg", None),
        P(),
        P(),
        P("dp", "seg", None),
        P("dp", "seg", None),
        P("dp", "seg", None),
        P("dp", "seg", None),
    )
    return jax.shard_map(
        local,
        mesh=mesh,
        in_specs=placed,
        out_specs=(
            P("dp", "seg", None),
            P("dp", "seg", None),
            P(("seg", "dp"), None),
            P(("seg", "dp")),
        ),
        check_vma=False,
    )
```

```python
import jax
import jax.numpy as jnp
from jax import lax
from jax.sharding import PartitionSpec as P

HEADS = 16
HEAD_DIM = 128


def passed_along(block, axis, distance):
    devices = range(lax.axis_size(axis))
    route = [(i - distance, i) for i in devices if i - distance in devices]
    return lax.ppermute(block, axis, route)


def mixing_of(query_rows, key_rows, summary_rows):
    trace_count, row_count, value_width = query_rows.shape
    slot_count = summary_rows.shape[1]
    query_heads = query_rows.reshape(trace_count, row_count, HEADS, HEAD_DIM)
    all_keys = jnp.concatenate([summary_rows, key_rows], axis=1)
    all_keys = all_keys.reshape(trace_count, slot_count + row_count, HEADS, HEAD_DIM)
    scores = jnp.einsum(
        "trhd,tkhd->thrk", query_heads, all_keys, preferred_element_type=jnp.float32
    )
    scores = scores * HEAD_DIM ** (-0.5)
    row_pos = lax.broadcasted_iota(jnp.int32, (row_count, slot_count + row_count), 0)
    col_pos = lax.broadcasted_iota(jnp.int32, (row_count, slot_count + row_count), 1)
    scores = jnp.where(col_pos <= row_pos + slot_count, scores, jnp.float32(-1e30))
    row_peak = jnp.max(scores, axis=-1, keepdims=True)
    exp_scores = jnp.exp(scores - row_peak)
    return (exp_scores / jnp.sum(exp_scores, axis=-1, keepdims=True)).astype(jnp.bfloat16)


def apply_map(matrix, state):
    return jnp.einsum("thkr,trhd->tkhd", matrix, state, precision=lax.Precision.HIGHEST)


def shifted(size, move):
    return [(i, move(i)) for i in range(size)]


def reduction_plan(seg_size, dp_size):
    x_n, z_n = seg_size // 4, dp_size // 2

    def y_move(sign):
        def move(i):
            s, d = divmod(i, dp_size)
            y = (2 * (d // z_n) + (s // 2) % 2 + sign) % 4
            return ((s // 4) * 4 + (y % 2) * 2 + s % 2) * dp_size + (y // 2) * z_n + d % z_n
        return move

    perms = {
        "x": [shifted(seg_size, lambda i, g=g: ((i // 4 + g) % x_n) * 4 + i % 4) for g in (1, -1, 2)],
        "z": [shifted(dp_size, lambda i, g=g: (i // z_n) * z_n + (i % z_n + g) % z_n) for g in (1, -1, 2)],
        "y": [shifted(seg_size * dp_size, y_move(g)) for g in (1, -1, 2)],
        "core": shifted(seg_size, lambda i: i ^ 1),
    }
    axes = {"x": "seg", "z": "dp", "y": ("seg", "dp")}
    return perms, axes


ORDERS = (("x", "y", "z"), ("y", "z", "x"), ("z", "x", "y"))


def feature_order(array, order, seg_size, dp_size):
    lead = array.shape[:-1]
    x_n, z_n = seg_size // 4, dp_size // 2
    split = array.reshape(*lead, x_n, 2, 2, 2, z_n, -1)
    n = len(lead)
    place = {"x": [n], "y": [n + 3, n + 1], "z": [n + 4], "core": [n + 2]}
    axes = list(range(n)) + place["core"] + [a for dim in order for a in place[dim]] + [n + 5]
    return split.transpose(axes).reshape(array.shape)


def reduce_colours(halves, where):
    perms, axes = reduction_plan(lax.axis_size("seg"), lax.axis_size("dp"))
    parts = [keep + lax.ppermute(send, "seg", perms["core"]) for keep, send in halves]
    for stage in range(3):
        dims = [order[stage] for order in ORDERS]
        moved = []
        for dim, part in zip(dims, parts):
            rows, cols = part.shape
            chunks = part.reshape(4, rows // 4, cols)

            def own(index, chunks=chunks):
                return lax.dynamic_index_in_dim(chunks, index % 4, 0, keepdims=False)

            coord = where[dim]
            sends = [
                lax.ppermute(own(coord + 1), axes[dim], perms[dim][0]),
                lax.ppermute(own(coord - 1), axes[dim], perms[dim][1]),
                lax.ppermute(own(coord + 2), axes[dim], perms[dim][2]),
            ]
            moved.append((own(coord), sends))
        moved = lax.optimization_barrier(moved)
        parts = [mine + sends[0] + sends[1] + sends[2] for mine, sends in moved]
    return parts


def local(hidden, norm_gain, value_weight, queries, token_keys, summary_keys, output_grad):
    trace_count, row_count, value_width = queries.shape
    slot_count = summary_keys.shape[1]
    model_width = hidden.shape[2]
    mixing = mixing_of(queries, token_keys, summary_keys)
    grad_heads = output_grad.reshape(trace_count, row_count, HEADS, HEAD_DIM)
    direct = jnp.einsum("thrk,trhd->tkhd", mixing, grad_heads, preferred_element_type=jnp.float32)
    slot_mixing = mixing[:, :, row_count - slot_count :, :].astype(jnp.float32)
    own_map = jnp.swapaxes(slot_mixing[..., :slot_count], 2, 3)
    own_offset = direct[:, :slot_count]

    chain_map, chain_offset = own_map, own_offset
    offset, seg_size = 1, lax.axis_size("seg")
    while offset < seg_size:
        last = 2 * offset >= seg_size
        far_offset = passed_along(chain_offset, "seg", -offset)
        new_offset = apply_map(chain_map, far_offset) + chain_offset
        if not last:
            far_map = passed_along(chain_map, "seg", -offset)
            chain_map = jnp.einsum(
                "thkm,thmr->thkr", chain_map, far_map, precision=lax.Precision.HIGHEST
            )
        chain_offset = new_offset
        offset *= 2
    summary_grad = chain_offset.reshape(trace_count, slot_count, value_width)
    incoming = passed_along(summary_grad, "seg", -1).reshape(chain_offset.shape)
    token_part = jnp.einsum(
        "thrk,trhd->tkhd", slot_mixing[..., slot_count:], incoming, precision=lax.Precision.HIGHEST
    )
    value_grad = (direct[:, slot_count:] + token_part).astype(jnp.bfloat16)
    value_grad = value_grad.reshape(trace_count * row_count, value_width)
    hidden_f = hidden.astype(jnp.float32)
    inv_rms = lax.rsqrt(jnp.mean(hidden_f * hidden_f, axis=-1, keepdims=True) + 1e-05)
    normed = hidden_f * inv_rms
    gain_f = norm_gain.astype(jnp.float32)
    scaled = (normed * gain_f).astype(jnp.bfloat16).reshape(trace_count * row_count, model_width)
    normalized_gradient = lax.dot_general(
        value_grad, value_weight, (((1,), (1,)), ((), ())), preferred_element_type=jnp.float32
    )
    normalized_gradient = normalized_gradient.reshape(trace_count, row_count, model_width)
    gain_grad = jnp.sum(
        (normalized_gradient * normed).reshape(trace_count * row_count, model_width), axis=0
    )
    scaled_grad = normalized_gradient * gain_f
    hidden_grad = inv_rms * (
        scaled_grad - normed * jnp.mean(scaled_grad * normed, axis=-1, keepdims=True)
    )
    seg_index, dp_index = lax.axis_index("seg"), lax.axis_index("dp")
    z_n = lax.axis_size("dp") // 2
    where = {
        "x": seg_index // 4,
        "y": 2 * (dp_index // z_n) + (seg_index // 2) % 2,
        "z": dp_index % z_n,
        "core": seg_index % 2,
    }
    seg_size, dp_size = lax.axis_size("seg"), lax.axis_size("dp")
    bounds = (0, 768, 1536, value_width)
    halves = []
    half = model_width // 2
    core = where["core"]
    for color, order in enumerate(ORDERS):
        columns = value_grad[:, bounds[color] : bounds[color + 1]]
        last = color == len(ORDERS) - 1
        if last:
            spare = jnp.zeros((columns.shape[0], 128), columns.dtype)
            columns = jnp.concatenate([columns, spare], axis=1)
            gain_col = feature_order(gain_grad, order, seg_size, dp_size)
        ordered = feature_order(scaled, order, seg_size, dp_size)
        pair = []
        for pick in (core, 1 - core):
            rows = lax.dynamic_slice_in_dim(ordered, pick * half, half, 1)
            part = lax.dot_general(
                rows, columns, (((0,), (0,)), ((), ())), preferred_element_type=jnp.float32
            )
            if last:
                lane = lax.broadcasted_iota(jnp.int32, part.shape, 1)
                gain_half = lax.dynamic_slice_in_dim(gain_col, pick * half, half, 0)
                gain_lane = part.shape[1] - 128
                part = part + jnp.where(lane == gain_lane, gain_half[:, None], jnp.float32(0))
            pair.append(part)
        halves.append(pair)
    pieces = reduce_colours(halves, where)
    both = jnp.concatenate(pieces, axis=1)
    weight_part, gain_part = both[:, :value_width], both[:, value_width]
    return (hidden_grad.astype(jnp.bfloat16), summary_grad, weight_part, gain_part)


def solution(mesh):
    placed = (
        P("dp", "seg", None),
        P(),
        P(),
        P("dp", "seg", None),
        P("dp", "seg", None),
        P("dp", "seg", None),
        P("dp", "seg", None),
    )
    return jax.shard_map(
        local,
        mesh=mesh,
        in_specs=placed,
        out_specs=(
            P("dp", "seg", None),
            P("dp", "seg", None),
            P(("seg", "dp"), None),
            P(("seg", "dp")),
        ),
        check_vma=False,
    )
```

```python
import jax
import jax.numpy as jnp
from jax import lax
from jax.sharding import PartitionSpec as P

HEADS = 16
HEAD_DIM = 128


def passed_along(block, axis, distance):
    devices = range(lax.axis_size(axis))
    route = [(i - distance, i) for i in devices if i - distance in devices]
    return lax.ppermute(block, axis, route)


def mixing_of(query_rows, key_rows, summary_rows):
    trace_count, row_count, value_width = query_rows.shape
    slot_count = summary_rows.shape[1]
    query_heads = query_rows.reshape(trace_count, row_count, HEADS, HEAD_DIM)
    all_keys = jnp.concatenate([summary_rows, key_rows], axis=1)
    all_keys = all_keys.reshape(trace_count, slot_count + row_count, HEADS, HEAD_DIM)
    scores = jnp.einsum(
        "trhd,tkhd->thrk", query_heads, all_keys, preferred_element_type=jnp.float32
    )
    scores = scores * HEAD_DIM ** (-0.5)
    row_pos = lax.broadcasted_iota(jnp.int32, (row_count, slot_count + row_count), 0)
    col_pos = lax.broadcasted_iota(jnp.int32, (row_count, slot_count + row_count), 1)
    scores = jnp.where(col_pos <= row_pos + slot_count, scores, jnp.float32(-1e30))
    row_peak = jnp.max(scores, axis=-1, keepdims=True)
    exp_scores = jnp.exp(scores - row_peak)
    return (exp_scores / jnp.sum(exp_scores, axis=-1, keepdims=True)).astype(jnp.bfloat16)


def apply_map(matrix, state):
    return jnp.einsum("thkr,trhd->tkhd", matrix, state, precision=lax.Precision.HIGHEST)


def shifted(size, move):
    return [(i, move(i)) for i in range(size)]


def reduction_plan(seg_size, dp_size):
    x_n, z_n = seg_size // 4, dp_size // 2

    def y_move(sign):
        def move(i):
            s, d = divmod(i, dp_size)
            y = (2 * (d // z_n) + (s // 2) % 2 + sign) % 4
            return ((s // 4) * 4 + (y % 2) * 2 + s % 2) * dp_size + (y // 2) * z_n + d % z_n
        return move

    perms = {
        "x": [shifted(seg_size, lambda i, g=g: ((i // 4 + g) % x_n) * 4 + i % 4) for g in (1, -1, 2)],
        "z": [shifted(dp_size, lambda i, g=g: (i // z_n) * z_n + (i % z_n + g) % z_n) for g in (1, -1, 2)],
        "y": [shifted(seg_size * dp_size, y_move(g)) for g in (1, -1, 2)],
        "core": shifted(seg_size, lambda i: i ^ 1),
    }
    axes = {"x": "seg", "z": "dp", "y": ("seg", "dp")}
    return perms, axes


ORDERS = (("x", "y", "z"), ("y", "z", "x"), ("z", "y", "x"))


def feature_order(array, order, seg_size, dp_size):
    lead = array.shape[:-1]
    x_n, z_n = seg_size // 4, dp_size // 2
    split = array.reshape(*lead, x_n, 2, 2, 2, z_n, -1)
    n = len(lead)
    place = {"x": [n], "y": [n + 3, n + 1], "z": [n + 4], "core": [n + 2]}
    axes = list(range(n)) + place["core"] + [a for dim in order for a in place[dim]] + [n + 5]
    return split.transpose(axes).reshape(array.shape)


def reduce_colours(halves, where):
    perms, axes = reduction_plan(lax.axis_size("seg"), lax.axis_size("dp"))
    parts = [keep + lax.ppermute(send, "seg", perms["core"]) for keep, send in halves]
    for stage in range(3):
        groups = {}
        for color, order in enumerate(ORDERS):
            groups.setdefault(order[stage], []).append(color)
        moved = []
        for dim, members in groups.items():
            part = jnp.concatenate([parts[c] for c in members], axis=1)
            rows, cols = part.shape
            chunks = part.reshape(4, rows // 4, cols)

            def own(index, chunks=chunks):
                return lax.dynamic_index_in_dim(chunks, index % 4, 0, keepdims=False)

            coord = where[dim]
            sends = [
                lax.ppermute(own(coord + 1), axes[dim], perms[dim][0]),
                lax.ppermute(own(coord - 1), axes[dim], perms[dim][1]),
                lax.ppermute(own(coord + 2), axes[dim], perms[dim][2]),
            ]
            moved.append((own(coord), sends))
        moved = lax.optimization_barrier(moved)
        for members, (mine, sends) in zip(groups.values(), moved):
            total = mine + sends[0] + sends[1] + sends[2]
            edge = 0
            for c in members:
                width = parts[c].shape[1]
                parts[c] = total[:, edge : edge + width]
                edge += width
    return parts


def local(hidden, norm_gain, value_weight, queries, token_keys, summary_keys, output_grad):
    trace_count, row_count, value_width = queries.shape
    slot_count = summary_keys.shape[1]
    model_width = hidden.shape[2]
    mixing = mixing_of(queries, token_keys, summary_keys)
    grad_heads = output_grad.reshape(trace_count, row_count, HEADS, HEAD_DIM)
    direct = jnp.einsum("thrk,trhd->tkhd", mixing, grad_heads, preferred_element_type=jnp.float32)
    slot_mixing = mixing[:, :, row_count - slot_count :, :].astype(jnp.float32)
    own_map = jnp.swapaxes(slot_mixing[..., :slot_count], 2, 3)
    own_offset = direct[:, :slot_count]

    chain_map, chain_offset = own_map, own_offset
    offset, seg_size = 1, lax.axis_size("seg")
    while offset < seg_size:
        last = 2 * offset >= seg_size
        far_offset = passed_along(chain_offset, "seg", -offset)
        new_offset = apply_map(chain_map, far_offset) + chain_offset
        if not last:
            far_map = passed_along(chain_map, "seg", -offset)
            chain_map = jnp.einsum(
                "thkm,thmr->thkr", chain_map, far_map, precision=lax.Precision.HIGHEST
            )
        chain_offset = new_offset
        offset *= 2
    summary_grad = chain_offset.reshape(trace_count, slot_count, value_width)
    incoming = passed_along(summary_grad, "seg", -1).reshape(chain_offset.shape)
    token_part = jnp.einsum(
        "thrk,trhd->tkhd", slot_mixing[..., slot_count:], incoming, precision=lax.Precision.HIGHEST
    )
    value_grad = (direct[:, slot_count:] + token_part).astype(jnp.bfloat16)
    value_grad = value_grad.reshape(trace_count * row_count, value_width)
    hidden_f = hidden.astype(jnp.float32)
    inv_rms = lax.rsqrt(jnp.mean(hidden_f * hidden_f, axis=-1, keepdims=True) + 1e-05)
    normed = hidden_f * inv_rms
    gain_f = norm_gain.astype(jnp.float32)
    scaled = (normed * gain_f).astype(jnp.bfloat16).reshape(trace_count * row_count, model_width)
    normalized_gradient = lax.dot_general(
        value_grad, value_weight, (((1,), (1,)), ((), ())), preferred_element_type=jnp.float32
    )
    normalized_gradient = normalized_gradient.reshape(trace_count, row_count, model_width)
    gain_grad = jnp.sum(
        (normalized_gradient * normed).reshape(trace_count * row_count, model_width), axis=0
    )
    scaled_grad = normalized_gradient * gain_f
    hidden_grad = inv_rms * (
        scaled_grad - normed * jnp.mean(scaled_grad * normed, axis=-1, keepdims=True)
    )
    seg_index, dp_index = lax.axis_index("seg"), lax.axis_index("dp")
    z_n = lax.axis_size("dp") // 2
    where = {
        "x": seg_index // 4,
        "y": 2 * (dp_index // z_n) + (seg_index // 2) % 2,
        "z": dp_index % z_n,
        "core": seg_index % 2,
    }
    seg_size, dp_size = lax.axis_size("seg"), lax.axis_size("dp")
    bounds = (0, 768, 1536, value_width)
    halves = []
    half = model_width // 2
    core = where["core"]
    for color, order in enumerate(ORDERS):
        columns = value_grad[:, bounds[color] : bounds[color + 1]]
        last = color == len(ORDERS) - 1
        if last:
            spare = jnp.zeros((columns.shape[0], 128), columns.dtype)
            columns = jnp.concatenate([columns, spare], axis=1)
            gain_col = feature_order(gain_grad, order, seg_size, dp_size)
        ordered = feature_order(scaled, order, seg_size, dp_size)
        pair = []
        for pick in (core, 1 - core):
            rows = lax.dynamic_slice_in_dim(ordered, pick * half, half, 1)
            part = lax.dot_general(
                rows, columns, (((0,), (0,)), ((), ())), preferred_element_type=jnp.float32
            )
            if last:
                lane = lax.broadcasted_iota(jnp.int32, part.shape, 1)
                gain_half = lax.dynamic_slice_in_dim(gain_col, pick * half, half, 0)
                gain_lane = part.shape[1] - 128
                part = part + jnp.where(lane == gain_lane, gain_half[:, None], jnp.float32(0))
            pair.append(part)
        halves.append(pair)
    pieces = reduce_colours(halves, where)
    both = jnp.concatenate(pieces, axis=1)
    weight_part, gain_part = both[:, :value_width], both[:, value_width]
    return (hidden_grad.astype(jnp.bfloat16), summary_grad, weight_part, gain_part)


def solution(mesh):
    placed = (
        P("dp", "seg", None),
        P(),
        P(),
        P("dp", "seg", None),
        P("dp", "seg", None),
        P("dp", "seg", None),
        P("dp", "seg", None),
    )
    return jax.shard_map(
        local,
        mesh=mesh,
        in_specs=placed,
        out_specs=(
            P("dp", "seg", None),
            P("dp", "seg", None),
            P(("seg", "dp"), None),
            P(("seg", "dp")),
        ),
        check_vma=False,
    )
```

```python
import jax
import jax.numpy as jnp
from jax import lax
from jax.sharding import PartitionSpec as P

HEADS = 16
HEAD_DIM = 128


def passed_along(block, axis, distance):
    devices = range(lax.axis_size(axis))
    route = [(i - distance, i) for i in devices if i - distance in devices]
    return lax.ppermute(block, axis, route)


def mixing_of(query_rows, key_rows, summary_rows):
    trace_count, row_count, value_width = query_rows.shape
    slot_count = summary_rows.shape[1]
    query_heads = query_rows.reshape(trace_count, row_count, HEADS, HEAD_DIM)
    all_keys = jnp.concatenate([summary_rows, key_rows], axis=1)
    all_keys = all_keys.reshape(trace_count, slot_count + row_count, HEADS, HEAD_DIM)
    scores = jnp.einsum(
        "trhd,tkhd->thrk", query_heads, all_keys, preferred_element_type=jnp.float32
    )
    scores = scores * HEAD_DIM ** (-0.5)
    row_pos = lax.broadcasted_iota(jnp.int32, (row_count, slot_count + row_count), 0)
    col_pos = lax.broadcasted_iota(jnp.int32, (row_count, slot_count + row_count), 1)
    scores = jnp.where(col_pos <= row_pos + slot_count, scores, jnp.float32(-1e30))
    row_peak = jnp.max(scores, axis=-1, keepdims=True)
    exp_scores = jnp.exp(scores - row_peak)
    return (exp_scores / jnp.sum(exp_scores, axis=-1, keepdims=True)).astype(jnp.bfloat16)


def apply_map(matrix, state):
    return jnp.einsum("thkr,trhd->tkhd", matrix, state, precision=lax.Precision.HIGHEST)


def shifted(size, move):
    return [(i, move(i)) for i in range(size)]


def reduction_plan(seg_size, dp_size):
    x_n, z_n = seg_size // 4, dp_size // 2

    def y_move(sign):
        def move(i):
            s, d = divmod(i, dp_size)
            y = (2 * (d // z_n) + (s // 2) % 2 + sign) % 4
            return ((s // 4) * 4 + (y % 2) * 2 + s % 2) * dp_size + (y // 2) * z_n + d % z_n
        return move

    perms = {
        "x": [shifted(seg_size, lambda i, g=g: ((i // 4 + g) % x_n) * 4 + i % 4) for g in (1, -1, 2)],
        "z": [shifted(dp_size, lambda i, g=g: (i // z_n) * z_n + (i % z_n + g) % z_n) for g in (1, -1, 2)],
        "y": [shifted(seg_size * dp_size, y_move(g)) for g in (1, -1, 2)],
        "core": shifted(seg_size, lambda i: i ^ 1),
    }
    axes = {"x": "seg", "z": "dp", "y": ("seg", "dp")}
    return perms, axes


ORDERS = (("x", "y", "z"), ("x", "y", "z"), ("x", "y", "z"))


def feature_order(array, order, seg_size, dp_size):
    lead = array.shape[:-1]
    x_n, z_n = seg_size // 4, dp_size // 2
    split = array.reshape(*lead, x_n, 2, 2, 2, z_n, -1)
    n = len(lead)
    place = {"x": [n], "y": [n + 3, n + 1], "z": [n + 4], "core": [n + 2]}
    axes = list(range(n)) + place["core"] + [a for dim in order for a in place[dim]] + [n + 5]
    return split.transpose(axes).reshape(array.shape)


def reduce_colours(halves, where):
    perms, axes = reduction_plan(lax.axis_size("seg"), lax.axis_size("dp"))
    parts = [keep + lax.ppermute(send, "seg", perms["core"]) for keep, send in halves]
    for stage in range(3):
        groups = {}
        for color, order in enumerate(ORDERS):
            groups.setdefault(order[stage], []).append(color)
        moved = []
        for dim, members in groups.items():
            part = jnp.concatenate([parts[c] for c in members], axis=1)
            rows, cols = part.shape
            chunks = part.reshape(4, rows // 4, cols)

            def own(index, chunks=chunks):
                return lax.dynamic_index_in_dim(chunks, index % 4, 0, keepdims=False)

            coord = where[dim]
            sends = [
                lax.ppermute(own(coord + 1), axes[dim], perms[dim][0]),
                lax.ppermute(own(coord - 1), axes[dim], perms[dim][1]),
                lax.ppermute(own(coord + 2), axes[dim], perms[dim][2]),
            ]
            moved.append((own(coord), sends))
        moved = lax.optimization_barrier(moved)
        for members, (mine, sends) in zip(groups.values(), moved):
            total = mine + sends[0] + sends[1] + sends[2]
            edge = 0
            for c in members:
                width = parts[c].shape[1]
                parts[c] = total[:, edge : edge + width]
                edge += width
    return parts


def local(hidden, norm_gain, value_weight, queries, token_keys, summary_keys, output_grad):
    trace_count, row_count, value_width = queries.shape
    slot_count = summary_keys.shape[1]
    model_width = hidden.shape[2]
    mixing = mixing_of(queries, token_keys, summary_keys)
    grad_heads = output_grad.reshape(trace_count, row_count, HEADS, HEAD_DIM)
    direct = jnp.einsum("thrk,trhd->tkhd", mixing, grad_heads, preferred_element_type=jnp.float32)
    slot_mixing = mixing[:, :, row_count - slot_count :, :].astype(jnp.float32)
    own_map = jnp.swapaxes(slot_mixing[..., :slot_count], 2, 3)
    own_offset = direct[:, :slot_count]

    chain_map, chain_offset = own_map, own_offset
    offset, seg_size = 1, lax.axis_size("seg")
    while offset < seg_size:
        last = 2 * offset >= seg_size
        far_offset = passed_along(chain_offset, "seg", -offset)
        new_offset = apply_map(chain_map, far_offset) + chain_offset
        if not last:
            far_map = passed_along(chain_map, "seg", -offset)
            chain_map = jnp.einsum(
                "thkm,thmr->thkr", chain_map, far_map, precision=lax.Precision.HIGHEST
            )
        chain_offset = new_offset
        offset *= 2
    summary_grad = chain_offset.reshape(trace_count, slot_count, value_width)
    incoming = passed_along(summary_grad, "seg", -1).reshape(chain_offset.shape)
    token_part = jnp.einsum(
        "thrk,trhd->tkhd", slot_mixing[..., slot_count:], incoming, precision=lax.Precision.HIGHEST
    )
    value_grad = (direct[:, slot_count:] + token_part).astype(jnp.bfloat16)
    value_grad = value_grad.reshape(trace_count * row_count, value_width)
    hidden_f = hidden.astype(jnp.float32)
    inv_rms = lax.rsqrt(jnp.mean(hidden_f * hidden_f, axis=-1, keepdims=True) + 1e-05)
    normed = hidden_f * inv_rms
    gain_f = norm_gain.astype(jnp.float32)
    scaled = (normed * gain_f).astype(jnp.bfloat16).reshape(trace_count * row_count, model_width)
    normalized_gradient = lax.dot_general(
        value_grad, value_weight, (((1,), (1,)), ((), ())), preferred_element_type=jnp.float32
    )
    normalized_gradient = normalized_gradient.reshape(trace_count, row_count, model_width)
    gain_grad = jnp.sum(
        (normalized_gradient * normed).reshape(trace_count * row_count, model_width), axis=0
    )
    scaled_grad = normalized_gradient * gain_f
    hidden_grad = inv_rms * (
        scaled_grad - normed * jnp.mean(scaled_grad * normed, axis=-1, keepdims=True)
    )
    seg_index, dp_index = lax.axis_index("seg"), lax.axis_index("dp")
    z_n = lax.axis_size("dp") // 2
    where = {
        "x": seg_index // 4,
        "y": 2 * (dp_index // z_n) + (seg_index // 2) % 2,
        "z": dp_index % z_n,
        "core": seg_index % 2,
    }
    seg_size, dp_size = lax.axis_size("seg"), lax.axis_size("dp")
    bounds = (0, 768, 1536, value_width)
    halves = []
    half = model_width // 2
    core = where["core"]
    for color, order in enumerate(ORDERS):
        columns = value_grad[:, bounds[color] : bounds[color + 1]]
        last = color == len(ORDERS) - 1
        if last:
            spare = jnp.zeros((columns.shape[0], 128), columns.dtype)
            columns = jnp.concatenate([columns, spare], axis=1)
            gain_col = feature_order(gain_grad, order, seg_size, dp_size)
        ordered = feature_order(scaled, order, seg_size, dp_size)
        pair = []
        for pick in (core, 1 - core):
            rows = lax.dynamic_slice_in_dim(ordered, pick * half, half, 1)
            part = lax.dot_general(
                rows, columns, (((0,), (0,)), ((), ())), preferred_element_type=jnp.float32
            )
            if last:
                lane = lax.broadcasted_iota(jnp.int32, part.shape, 1)
                gain_half = lax.dynamic_slice_in_dim(gain_col, pick * half, half, 0)
                gain_lane = part.shape[1] - 128
                part = part + jnp.where(lane == gain_lane, gain_half[:, None], jnp.float32(0))
            pair.append(part)
        halves.append(pair)
    pieces = reduce_colours(halves, where)
    both = jnp.concatenate(pieces, axis=1)
    weight_part, gain_part = both[:, :value_width], both[:, value_width]
    return (hidden_grad.astype(jnp.bfloat16), summary_grad, weight_part, gain_part)


def solution(mesh):
    placed = (
        P("dp", "seg", None),
        P(),
        P(),
        P("dp", "seg", None),
        P("dp", "seg", None),
        P("dp", "seg", None),
        P("dp", "seg", None),
    )
    return jax.shard_map(
        local,
        mesh=mesh,
        in_specs=placed,
        out_specs=(
            P("dp", "seg", None),
            P("dp", "seg", None),
            P(("seg", "dp"), None),
            P(("seg", "dp")),
        ),
        check_vma=False,
    )
```

```python
import jax
import jax.numpy as jnp
from jax import lax
from jax.sharding import PartitionSpec as P

HEADS = 16
HEAD_DIM = 128


def passed_along(block, axis, distance):
    devices = range(lax.axis_size(axis))
    route = [(i - distance, i) for i in devices if i - distance in devices]
    return lax.ppermute(block, axis, route)


def mixing_of(query_rows, key_rows, summary_rows):
    trace_count, row_count, value_width = query_rows.shape
    slot_count = summary_rows.shape[1]
    query_heads = query_rows.reshape(trace_count, row_count, HEADS, HEAD_DIM)
    all_keys = jnp.concatenate([summary_rows, key_rows], axis=1)
    all_keys = all_keys.reshape(trace_count, slot_count + row_count, HEADS, HEAD_DIM)
    scores = jnp.einsum(
        "trhd,tkhd->thrk", query_heads, all_keys, preferred_element_type=jnp.float32
    )
    scores = scores * HEAD_DIM ** (-0.5)
    row_pos = lax.broadcasted_iota(jnp.int32, (row_count, slot_count + row_count), 0)
    col_pos = lax.broadcasted_iota(jnp.int32, (row_count, slot_count + row_count), 1)
    scores = jnp.where(col_pos <= row_pos + slot_count, scores, jnp.float32(-1e30))
    row_peak = jnp.max(scores, axis=-1, keepdims=True)
    exp_scores = jnp.exp(scores - row_peak)
    return (exp_scores / jnp.sum(exp_scores, axis=-1, keepdims=True)).astype(jnp.bfloat16)


def apply_map(matrix, state):
    return jnp.einsum("thkr,trhd->tkhd", matrix, state, precision=lax.Precision.HIGHEST)


def shifted(size, move):
    return [(i, move(i)) for i in range(size)]


def reduction_plan(seg_size, dp_size):
    x_n, z_n = seg_size // 4, dp_size // 2

    def y_move(sign):
        def move(i):
            s, d = divmod(i, dp_size)
            y = (2 * (d // z_n) + (s // 2) % 2 + sign) % 4
            return ((s // 4) * 4 + (y % 2) * 2 + s % 2) * dp_size + (y // 2) * z_n + d % z_n
        return move

    perms = {
        "x": [shifted(seg_size, lambda i, g=g: ((i // 4 + g) % x_n) * 4 + i % 4) for g in (1, -1, 2)],
        "z": [shifted(dp_size, lambda i, g=g: (i // z_n) * z_n + (i % z_n + g) % z_n) for g in (1, -1, 2)],
        "y": [shifted(seg_size * dp_size, y_move(g)) for g in (1, -1, 2)],
        "core": shifted(seg_size, lambda i: i ^ 1),
    }
    axes = {"x": "seg", "z": "dp", "y": ("seg", "dp")}
    return perms, axes


ORDERS = (("x", "y", "z"), ("y", "z", "x"), ("z", "y", "x"))


def feature_order(array, order, seg_size, dp_size):
    lead = array.shape[:-1]
    x_n, z_n = seg_size // 4, dp_size // 2
    split = array.reshape(*lead, x_n, 2, 2, 2, z_n, -1)
    n = len(lead)
    place = {"x": [n], "y": [n + 3, n + 1], "z": [n + 4], "core": [n + 2]}
    axes = list(range(n)) + place["core"] + [a for dim in order for a in place[dim]] + [n + 5]
    return split.transpose(axes).reshape(array.shape)


def ring_first_stage(parts, where, perms, axes):
    dims = [order[0] for order in ORDERS]
    split = []
    for part in parts:
        rows, cols = part.shape
        quarter = part.reshape(4, 2, rows // 8, cols)
        split.append((quarter[:, 0], quarter[:, 1]))

    def own(block, index):
        return lax.dynamic_index_in_dim(block, index % 4, 0, keepdims=False)

    acc = [
        (own(ahead, where[dim] - 1), own(behind, where[dim] + 1))
        for dim, (ahead, behind) in zip(dims, split)
    ]
    for step in (2, 3, 4):
        moved = [
            (lax.ppermute(a, axes[dim], perms[dim][0]), lax.ppermute(b, axes[dim], perms[dim][1]))
            for dim, (a, b) in zip(dims, acc)
        ]
        moved = lax.optimization_barrier(moved)
        acc = [
            (a + own(ahead, where[dim] - step), b + own(behind, where[dim] + step))
            for dim, (a, b), (ahead, behind) in zip(dims, moved, split)
        ]
    return [jnp.concatenate(pair, axis=0) for pair in acc]


def reduce_colours(halves, where):
    perms, axes = reduction_plan(lax.axis_size("seg"), lax.axis_size("dp"))
    parts = [keep + lax.ppermute(send, "seg", perms["core"]) for keep, send in halves]
    parts = ring_first_stage(parts, where, perms, axes)
    for stage in range(1, 3):
        groups = {}
        for color, order in enumerate(ORDERS):
            groups.setdefault(order[stage], []).append(color)
        moved = []
        for dim, members in groups.items():
            part = jnp.concatenate([parts[c] for c in members], axis=1)
            rows, cols = part.shape
            chunks = part.reshape(4, rows // 4, cols)

            def own(index, chunks=chunks):
                return lax.dynamic_index_in_dim(chunks, index % 4, 0, keepdims=False)

            coord = where[dim]
            sends = [
                lax.ppermute(own(coord + 1), axes[dim], perms[dim][0]),
                lax.ppermute(own(coord - 1), axes[dim], perms[dim][1]),
                lax.ppermute(own(coord + 2), axes[dim], perms[dim][2]),
            ]
            moved.append((own(coord), sends))
        moved = lax.optimization_barrier(moved)
        for members, (mine, sends) in zip(groups.values(), moved):
            total = mine + sends[0] + sends[1] + sends[2]
            edge = 0
            for c in members:
                width = parts[c].shape[1]
                parts[c] = total[:, edge : edge + width]
                edge += width
    return parts


def local(hidden, norm_gain, value_weight, queries, token_keys, summary_keys, output_grad):
    trace_count, row_count, value_width = queries.shape
    slot_count = summary_keys.shape[1]
    model_width = hidden.shape[2]
    mixing = mixing_of(queries, token_keys, summary_keys)
    grad_heads = output_grad.reshape(trace_count, row_count, HEADS, HEAD_DIM)
    direct = jnp.einsum("thrk,trhd->tkhd", mixing, grad_heads, preferred_element_type=jnp.float32)
    slot_mixing = mixing[:, :, row_count - slot_count :, :].astype(jnp.float32)
    own_map = jnp.swapaxes(slot_mixing[..., :slot_count], 2, 3)
    own_offset = direct[:, :slot_count]

    chain_map, chain_offset = own_map, own_offset
    offset, seg_size = 1, lax.axis_size("seg")
    while offset < seg_size:
        last = 2 * offset >= seg_size
        far_offset = passed_along(chain_offset, "seg", -offset)
        new_offset = apply_map(chain_map, far_offset) + chain_offset
        if not last:
            far_map = passed_along(chain_map, "seg", -offset)
            chain_map = jnp.einsum(
                "thkm,thmr->thkr", chain_map, far_map, precision=lax.Precision.HIGHEST
            )
        chain_offset = new_offset
        offset *= 2
    summary_grad = chain_offset.reshape(trace_count, slot_count, value_width)
    incoming = passed_along(summary_grad, "seg", -1).reshape(chain_offset.shape)
    token_part = jnp.einsum(
        "thrk,trhd->tkhd", slot_mixing[..., slot_count:], incoming, precision=lax.Precision.HIGHEST
    )
    value_grad = (direct[:, slot_count:] + token_part).astype(jnp.bfloat16)
    value_grad = value_grad.reshape(trace_count * row_count, value_width)
    hidden_f = hidden.astype(jnp.float32)
    inv_rms = lax.rsqrt(jnp.mean(hidden_f * hidden_f, axis=-1, keepdims=True) + 1e-05)
    normed = hidden_f * inv_rms
    gain_f = norm_gain.astype(jnp.float32)
    scaled = (normed * gain_f).astype(jnp.bfloat16).reshape(trace_count * row_count, model_width)
    normalized_gradient = lax.dot_general(
        value_grad, value_weight, (((1,), (1,)), ((), ())), preferred_element_type=jnp.float32
    )
    normalized_gradient = normalized_gradient.reshape(trace_count, row_count, model_width)
    gain_grad = jnp.sum(
        (normalized_gradient * normed).reshape(trace_count * row_count, model_width), axis=0
    )
    scaled_grad = normalized_gradient * gain_f
    hidden_grad = inv_rms * (
        scaled_grad - normed * jnp.mean(scaled_grad * normed, axis=-1, keepdims=True)
    )
    seg_index, dp_index = lax.axis_index("seg"), lax.axis_index("dp")
    z_n = lax.axis_size("dp") // 2
    where = {
        "x": seg_index // 4,
        "y": 2 * (dp_index // z_n) + (seg_index // 2) % 2,
        "z": dp_index % z_n,
        "core": seg_index % 2,
    }
    seg_size, dp_size = lax.axis_size("seg"), lax.axis_size("dp")
    bounds = (0, 768, 1536, value_width)
    halves = []
    half = model_width // 2
    core = where["core"]
    for color, order in enumerate(ORDERS):
        columns = value_grad[:, bounds[color] : bounds[color + 1]]
        last = color == len(ORDERS) - 1
        if last:
            spare = jnp.zeros((columns.shape[0], 128), columns.dtype)
            columns = jnp.concatenate([columns, spare], axis=1)
            gain_col = feature_order(gain_grad, order, seg_size, dp_size)
        ordered = feature_order(scaled, order, seg_size, dp_size)
        pair = []
        for pick in (core, 1 - core):
            rows = lax.dynamic_slice_in_dim(ordered, pick * half, half, 1)
            part = lax.dot_general(
                rows, columns, (((0,), (0,)), ((), ())), preferred_element_type=jnp.float32
            )
            if last:
                lane = lax.broadcasted_iota(jnp.int32, part.shape, 1)
                gain_half = lax.dynamic_slice_in_dim(gain_col, pick * half, half, 0)
                gain_lane = part.shape[1] - 128
                part = part + jnp.where(lane == gain_lane, gain_half[:, None], jnp.float32(0))
            pair.append(part)
        halves.append(pair)
    pieces = reduce_colours(halves, where)
    both = jnp.concatenate(pieces, axis=1)
    weight_part, gain_part = both[:, :value_width], both[:, value_width]
    return (hidden_grad.astype(jnp.bfloat16), summary_grad, weight_part, gain_part)


def solution(mesh):
    placed = (
        P("dp", "seg", None),
        P(),
        P(),
        P("dp", "seg", None),
        P("dp", "seg", None),
        P("dp", "seg", None),
        P("dp", "seg", None),
    )
    return jax.shard_map(
        local,
        mesh=mesh,
        in_specs=placed,
        out_specs=(
            P("dp", "seg", None),
            P("dp", "seg", None),
            P(("seg", "dp"), None),
            P(("seg", "dp")),
        ),
        check_vma=False,
    )
```

```python
import jax
import jax.numpy as jnp
from jax import lax
from jax.sharding import PartitionSpec as P

HEADS = 16
HEAD_DIM = 128


def passed_along(block, axis, distance):
    devices = range(lax.axis_size(axis))
    route = [(i - distance, i) for i in devices if i - distance in devices]
    return lax.ppermute(block, axis, route)


def mixing_of(query_rows, key_rows, summary_rows):
    trace_count, row_count, value_width = query_rows.shape
    slot_count = summary_rows.shape[1]
    query_heads = query_rows.reshape(trace_count, row_count, HEADS, HEAD_DIM)
    all_keys = jnp.concatenate([summary_rows, key_rows], axis=1)
    all_keys = all_keys.reshape(trace_count, slot_count + row_count, HEADS, HEAD_DIM)
    scores = jnp.einsum(
        "trhd,tkhd->thrk", query_heads, all_keys, preferred_element_type=jnp.float32
    )
    scores = scores * HEAD_DIM ** (-0.5)
    row_pos = lax.broadcasted_iota(jnp.int32, (row_count, slot_count + row_count), 0)
    col_pos = lax.broadcasted_iota(jnp.int32, (row_count, slot_count + row_count), 1)
    scores = jnp.where(col_pos <= row_pos + slot_count, scores, jnp.float32(-1e30))
    row_peak = jnp.max(scores, axis=-1, keepdims=True)
    exp_scores = jnp.exp(scores - row_peak)
    return (exp_scores / jnp.sum(exp_scores, axis=-1, keepdims=True)).astype(jnp.bfloat16)


def apply_map(matrix, state):
    return jnp.einsum("thkr,trhd->tkhd", matrix, state, precision=lax.Precision.HIGHEST)


def shifted(size, move):
    return [(i, move(i)) for i in range(size)]


def reduction_plan(seg_size, dp_size):
    x_n, z_n = seg_size // 4, dp_size // 2

    def y_move(sign):
        def move(i):
            s, d = divmod(i, dp_size)
            y = (2 * (d // z_n) + (s // 2) % 2 + sign) % 4
            return ((s // 4) * 4 + (y % 2) * 2 + s % 2) * dp_size + (y // 2) * z_n + d % z_n
        return move

    perms = {
        "x": [shifted(seg_size, lambda i, g=g: ((i // 4 + g) % x_n) * 4 + i % 4) for g in (1, -1, 2)],
        "z": [shifted(dp_size, lambda i, g=g: (i // z_n) * z_n + (i % z_n + g) % z_n) for g in (1, -1, 2)],
        "y": [shifted(seg_size * dp_size, y_move(g)) for g in (1, -1, 2)],
        "core": shifted(seg_size, lambda i: i ^ 1),
    }
    axes = {"x": "seg", "z": "dp", "y": ("seg", "dp")}
    return perms, axes


ORDERS = (("x", "y", "z"), ("y", "z", "x"), ("z", "y", "x"))


def feature_order(array, order, seg_size, dp_size):
    lead = array.shape[:-1]
    x_n, z_n = seg_size // 4, dp_size // 2
    split = array.reshape(*lead, x_n, 2, 2, 2, z_n, -1)
    n = len(lead)
    place = {"x": [n], "y": [n + 3, n + 1], "z": [n + 4], "core": [n + 2]}
    axes = list(range(n)) + place["core"] + [a for dim in order for a in place[dim]] + [n + 5]
    return split.transpose(axes).reshape(array.shape)


def ring_first_stage(parts, where, perms, axes):
    dims = [order[0] for order in ORDERS]
    split = []
    for part in parts:
        rows, cols = part.shape
        quarter = part.reshape(4, 2, rows // 8, cols)
        split.append((quarter[:, 0], quarter[:, 1]))

    def own(block, index):
        return lax.dynamic_index_in_dim(block, index % 4, 0, keepdims=False)

    acc = [
        (own(ahead, where[dim] - 1), own(behind, where[dim] + 1))
        for dim, (ahead, behind) in zip(dims, split)
    ]
    for step in (2, 3, 4):
        moved = [
            (lax.ppermute(a, axes[dim], perms[dim][0]), lax.ppermute(b, axes[dim], perms[dim][1]))
            for dim, (a, b) in zip(dims, acc)
        ]
        moved = lax.optimization_barrier(moved)
        acc = [
            (a + own(ahead, where[dim] - step), b + own(behind, where[dim] + step))
            for dim, (a, b), (ahead, behind) in zip(dims, moved, split)
        ]
    return [jnp.concatenate(pair, axis=0) for pair in acc]


def reduce_colours(halves, where):
    perms, axes = reduction_plan(lax.axis_size("seg"), lax.axis_size("dp"))
    parts = [keep + lax.ppermute(send, "seg", perms["core"]) for keep, send in halves]
    parts = ring_first_stage(parts, where, perms, axes)
    for stage in range(1, 3):
        groups = {}
        for color, order in enumerate(ORDERS):
            groups.setdefault(order[stage], []).append(color)
        moved = []
        for dim, members in groups.items():
            part = jnp.concatenate([parts[c] for c in members], axis=1)
            rows, cols = part.shape
            chunks = part.reshape(4, rows // 4, cols)

            def own(index, chunks=chunks):
                return lax.dynamic_index_in_dim(chunks, index % 4, 0, keepdims=False)

            coord = where[dim]
            sends = [
                lax.ppermute(own(coord + 1), axes[dim], perms[dim][0]),
                lax.ppermute(own(coord - 1), axes[dim], perms[dim][1]),
                lax.ppermute(own(coord + 2), axes[dim], perms[dim][2]),
            ]
            moved.append((own(coord), sends))
        moved = lax.optimization_barrier(moved)
        for members, (mine, sends) in zip(groups.values(), moved):
            total = mine + sends[0] + sends[1] + sends[2]
            edge = 0
            for c in members:
                width = parts[c].shape[1]
                parts[c] = total[:, edge : edge + width]
                edge += width
    return parts


def local(hidden, norm_gain, value_weight, queries, token_keys, summary_keys, output_grad):
    trace_count, row_count, value_width = queries.shape
    slot_count = summary_keys.shape[1]
    model_width = hidden.shape[2]
    mixing = mixing_of(queries, token_keys, summary_keys)
    grad_heads = output_grad.reshape(trace_count, row_count, HEADS, HEAD_DIM)
    direct = jnp.einsum("thrk,trhd->tkhd", mixing, grad_heads, preferred_element_type=jnp.float32)
    slot_mixing = mixing[:, :, row_count - slot_count :, :].astype(jnp.float32)
    own_map = jnp.swapaxes(slot_mixing[..., :slot_count], 2, 3)
    own_offset = direct[:, :slot_count]

    chain_map, chain_offset = own_map, own_offset
    offset, seg_size = 1, lax.axis_size("seg")
    while offset < seg_size:
        last = 2 * offset >= seg_size
        if last:
            far_offset = passed_along(chain_offset, "seg", -offset)
        else:
            flat_map = chain_map.reshape(-1)
            map_rows = -(-flat_map.size // value_width)
            flat_map = jnp.pad(flat_map, (0, map_rows * value_width - flat_map.size))
            packed = jnp.concatenate(
                [chain_offset.reshape(-1, value_width), flat_map.reshape(map_rows, value_width)]
            )
            far = passed_along(packed, "seg", -offset)
            far_offset = far[: -map_rows].reshape(chain_offset.shape)
            far_map = far[-map_rows:].reshape(-1)[: chain_map.size].reshape(chain_map.shape)
        new_offset = apply_map(chain_map, far_offset) + chain_offset
        if not last:
            chain_map = jnp.einsum(
                "thkm,thmr->thkr", chain_map, far_map, precision=lax.Precision.HIGHEST
            )
        chain_offset = new_offset
        offset *= 2
    summary_grad = chain_offset.reshape(trace_count, slot_count, value_width)
    incoming = passed_along(summary_grad, "seg", -1).reshape(chain_offset.shape)
    token_part = jnp.einsum(
        "thrk,trhd->tkhd", slot_mixing[..., slot_count:], incoming, precision=lax.Precision.HIGHEST
    )
    value_grad = (direct[:, slot_count:] + token_part).astype(jnp.bfloat16)
    value_grad = value_grad.reshape(trace_count * row_count, value_width)
    hidden_f = hidden.astype(jnp.float32)
    inv_rms = lax.rsqrt(jnp.mean(hidden_f * hidden_f, axis=-1, keepdims=True) + 1e-05)
    normed = hidden_f * inv_rms
    gain_f = norm_gain.astype(jnp.float32)
    scaled = (normed * gain_f).astype(jnp.bfloat16).reshape(trace_count * row_count, model_width)
    normalized_gradient = lax.dot_general(
        value_grad, value_weight, (((1,), (1,)), ((), ())), preferred_element_type=jnp.float32
    )
    normalized_gradient = normalized_gradient.reshape(trace_count, row_count, model_width)
    gain_grad = jnp.sum(
        (normalized_gradient * normed).reshape(trace_count * row_count, model_width), axis=0
    )
    scaled_grad = normalized_gradient * gain_f
    hidden_grad = inv_rms * (
        scaled_grad - normed * jnp.mean(scaled_grad * normed, axis=-1, keepdims=True)
    )
    seg_index, dp_index = lax.axis_index("seg"), lax.axis_index("dp")
    z_n = lax.axis_size("dp") // 2
    where = {
        "x": seg_index // 4,
        "y": 2 * (dp_index // z_n) + (seg_index // 2) % 2,
        "z": dp_index % z_n,
        "core": seg_index % 2,
    }
    seg_size, dp_size = lax.axis_size("seg"), lax.axis_size("dp")
    bounds = (0, 768, 1536, value_width)
    halves = []
    half = model_width // 2
    core = where["core"]
    for color, order in enumerate(ORDERS):
        columns = value_grad[:, bounds[color] : bounds[color + 1]]
        last = color == len(ORDERS) - 1
        if last:
            spare = jnp.zeros((columns.shape[0], 128), columns.dtype)
            columns = jnp.concatenate([columns, spare], axis=1)
            gain_col = feature_order(gain_grad, order, seg_size, dp_size)
        ordered = feature_order(scaled, order, seg_size, dp_size)
        pair = []
        for pick in (core, 1 - core):
            rows = lax.dynamic_slice_in_dim(ordered, pick * half, half, 1)
            part = lax.dot_general(
                rows, columns, (((0,), (0,)), ((), ())), preferred_element_type=jnp.float32
            )
            if last:
                lane = lax.broadcasted_iota(jnp.int32, part.shape, 1)
                gain_half = lax.dynamic_slice_in_dim(gain_col, pick * half, half, 0)
                gain_lane = part.shape[1] - 128
                part = part + jnp.where(lane == gain_lane, gain_half[:, None], jnp.float32(0))
            pair.append(part)
        halves.append(pair)
    pieces = reduce_colours(halves, where)
    both = jnp.concatenate(pieces, axis=1)
    weight_part, gain_part = both[:, :value_width], both[:, value_width]
    return (hidden_grad.astype(jnp.bfloat16), summary_grad, weight_part, gain_part)


def solution(mesh):
    placed = (
        P("dp", "seg", None),
        P(),
        P(),
        P("dp", "seg", None),
        P("dp", "seg", None),
        P("dp", "seg", None),
        P("dp", "seg", None),
    )
    return jax.shard_map(
        local,
        mesh=mesh,
        in_specs=placed,
        out_specs=(
            P("dp", "seg", None),
            P("dp", "seg", None),
            P(("seg", "dp"), None),
            P(("seg", "dp")),
        ),
        check_vma=False,
    )
```

```python
import jax
import jax.numpy as jnp
from jax import lax
from jax.sharding import PartitionSpec as P

HEADS = 16
HEAD_DIM = 128


def passed_along(block, axis, distance):
    devices = range(lax.axis_size(axis))
    route = [(i - distance, i) for i in devices if i - distance in devices]
    return lax.ppermute(block, axis, route)


def mixing_of(query_rows, key_rows, summary_rows):
    trace_count, row_count, value_width = query_rows.shape
    slot_count = summary_rows.shape[1]
    query_heads = query_rows.reshape(trace_count, row_count, HEADS, HEAD_DIM)
    all_keys = jnp.concatenate([summary_rows, key_rows], axis=1)
    all_keys = all_keys.reshape(trace_count, slot_count + row_count, HEADS, HEAD_DIM)
    scores = jnp.einsum(
        "trhd,tkhd->thrk", query_heads, all_keys, preferred_element_type=jnp.float32
    )
    scores = scores * HEAD_DIM ** (-0.5)
    row_pos = lax.broadcasted_iota(jnp.int32, (row_count, slot_count + row_count), 0)
    col_pos = lax.broadcasted_iota(jnp.int32, (row_count, slot_count + row_count), 1)
    scores = jnp.where(col_pos <= row_pos + slot_count, scores, jnp.float32(-1e30))
    row_peak = jnp.max(scores, axis=-1, keepdims=True)
    exp_scores = jnp.exp(scores - row_peak)
    return (exp_scores / jnp.sum(exp_scores, axis=-1, keepdims=True)).astype(jnp.bfloat16)


def apply_map(matrix, state):
    return jnp.einsum("thkr,trhd->tkhd", matrix, state, precision=lax.Precision.HIGHEST)


def shifted(size, move):
    return [(i, move(i)) for i in range(size)]


def reduction_plan(seg_size, dp_size):
    x_n, z_n = seg_size // 4, dp_size // 2

    def y_move(sign):
        def move(i):
            s, d = divmod(i, dp_size)
            y = (2 * (d // z_n) + (s // 2) % 2 + sign) % 4
            return ((s // 4) * 4 + (y % 2) * 2 + s % 2) * dp_size + (y // 2) * z_n + d % z_n
        return move

    perms = {
        "x": [shifted(seg_size, lambda i, g=g: ((i // 4 + g) % x_n) * 4 + i % 4) for g in (1, -1, 2)],
        "z": [shifted(dp_size, lambda i, g=g: (i // z_n) * z_n + (i % z_n + g) % z_n) for g in (1, -1, 2)],
        "y": [shifted(seg_size * dp_size, y_move(g)) for g in (1, -1, 2)],
        "core": shifted(seg_size, lambda i: i ^ 1),
    }
    axes = {"x": "seg", "z": "dp", "y": ("seg", "dp")}
    return perms, axes


ORDERS = (("x", "y", "z"), ("y", "z", "x"), ("z", "y", "x"))


def feature_order(array, order, seg_size, dp_size):
    lead = array.shape[:-1]
    x_n, z_n = seg_size // 4, dp_size // 2
    split = array.reshape(*lead, x_n, 2, 2, 2, z_n, -1)
    n = len(lead)
    place = {"x": [n], "y": [n + 3, n + 1], "z": [n + 4], "core": [n + 2]}
    axes = list(range(n)) + place["core"] + [a for dim in order for a in place[dim]] + [n + 5]
    return split.transpose(axes).reshape(array.shape)


def ring_first_stage(parts, where, perms, axes):
    dims = [order[0] for order in ORDERS]
    split = []
    for part in parts:
        rows, cols = part.shape
        quarter = part.reshape(4, 2, rows // 8, cols)
        split.append((quarter[:, 0], quarter[:, 1]))

    def own(block, index):
        return lax.dynamic_index_in_dim(block, index % 4, 0, keepdims=False)

    acc = [
        (own(ahead, where[dim] - 1), own(behind, where[dim] + 1))
        for dim, (ahead, behind) in zip(dims, split)
    ]
    for step in (2, 3, 4):
        moved = [
            (lax.ppermute(a, axes[dim], perms[dim][0]), lax.ppermute(b, axes[dim], perms[dim][1]))
            for dim, (a, b) in zip(dims, acc)
        ]
        moved = lax.optimization_barrier(moved)
        acc = [
            (a + own(ahead, where[dim] - step), b + own(behind, where[dim] + step))
            for dim, (a, b), (ahead, behind) in zip(dims, moved, split)
        ]
    return [jnp.concatenate(pair, axis=0) for pair in acc]


def reduce_colours(halves, where):
    perms, axes = reduction_plan(lax.axis_size("seg"), lax.axis_size("dp"))
    parts = [keep + lax.ppermute(send, "seg", perms["core"]) for keep, send in halves]
    parts = ring_first_stage(parts, where, perms, axes)
    for stage in range(1, 3):
        groups = {}
        for color, order in enumerate(ORDERS):
            groups.setdefault(order[stage], []).append(color)
        moved = []
        for dim, members in groups.items():
            part = jnp.concatenate([parts[c] for c in members], axis=1)
            rows, cols = part.shape
            chunks = part.reshape(4, rows // 4, cols)

            def own(index, chunks=chunks):
                return lax.dynamic_index_in_dim(chunks, index % 4, 0, keepdims=False)

            coord = where[dim]
            sends = [
                lax.ppermute(own(coord + 1), axes[dim], perms[dim][0]),
                lax.ppermute(own(coord - 1), axes[dim], perms[dim][1]),
                lax.ppermute(own(coord + 2), axes[dim], perms[dim][2]),
            ]
            moved.append((own(coord), sends))
        moved = lax.optimization_barrier(moved)
        for members, (mine, sends) in zip(groups.values(), moved):
            total = mine + sends[0] + sends[1] + sends[2]
            edge = 0
            for c in members:
                width = parts[c].shape[1]
                parts[c] = total[:, edge : edge + width]
                edge += width
    return parts


def local(hidden, norm_gain, value_weight, queries, token_keys, summary_keys, output_grad):
    trace_count, row_count, value_width = queries.shape
    slot_count = summary_keys.shape[1]
    model_width = hidden.shape[2]
    mixing = mixing_of(queries, token_keys, summary_keys)
    grad_heads = output_grad.reshape(trace_count, row_count, HEADS, HEAD_DIM)
    direct = jnp.einsum("thrk,trhd->tkhd", mixing, grad_heads, preferred_element_type=jnp.float32)
    slot_mixing = mixing[:, :, row_count - slot_count :, :].astype(jnp.float32)
    own_map = jnp.swapaxes(slot_mixing[..., :slot_count], 2, 3)
    own_offset = direct[:, :slot_count]

    chain_map, chain_offset = own_map, own_offset
    offset, seg_size = 1, lax.axis_size("seg")
    while 2 * offset < seg_size:
        far_offset = passed_along(chain_offset, "seg", -offset)
        far_map = passed_along(chain_map, "seg", -offset)
        chain_offset = apply_map(chain_map, far_offset) + chain_offset
        chain_map = jnp.einsum(
            "thkm,thmr->thkr", chain_map, far_map, precision=lax.Precision.HIGHEST
        )
        offset *= 2
    past_half = passed_along(chain_offset, "seg", -offset)
    past_next_half = passed_along(chain_offset, "seg", -offset - 1)
    next_map = passed_along(chain_map, "seg", -1)
    next_offset = passed_along(chain_offset, "seg", -1)
    summary_state = apply_map(chain_map, past_half) + chain_offset
    incoming = apply_map(next_map, past_next_half) + next_offset
    summary_grad = summary_state.reshape(trace_count, slot_count, value_width)
    token_part = jnp.einsum(
        "thrk,trhd->tkhd", slot_mixing[..., slot_count:], incoming, precision=lax.Precision.HIGHEST
    )
    value_grad = (direct[:, slot_count:] + token_part).astype(jnp.bfloat16)
    value_grad = value_grad.reshape(trace_count * row_count, value_width)
    hidden_f = hidden.astype(jnp.float32)
    inv_rms = lax.rsqrt(jnp.mean(hidden_f * hidden_f, axis=-1, keepdims=True) + 1e-05)
    normed = hidden_f * inv_rms
    gain_f = norm_gain.astype(jnp.float32)
    scaled = (normed * gain_f).astype(jnp.bfloat16).reshape(trace_count * row_count, model_width)
    normalized_gradient = lax.dot_general(
        value_grad, value_weight, (((1,), (1,)), ((), ())), preferred_element_type=jnp.float32
    )
    normalized_gradient = normalized_gradient.reshape(trace_count, row_count, model_width)
    gain_grad = jnp.sum(
        (normalized_gradient * normed).reshape(trace_count * row_count, model_width), axis=0
    )
    scaled_grad = normalized_gradient * gain_f
    hidden_grad = inv_rms * (
        scaled_grad - normed * jnp.mean(scaled_grad * normed, axis=-1, keepdims=True)
    )
    seg_index, dp_index = lax.axis_index("seg"), lax.axis_index("dp")
    z_n = lax.axis_size("dp") // 2
    where = {
        "x": seg_index // 4,
        "y": 2 * (dp_index // z_n) + (seg_index // 2) % 2,
        "z": dp_index % z_n,
        "core": seg_index % 2,
    }
    seg_size, dp_size = lax.axis_size("seg"), lax.axis_size("dp")
    bounds = (0, 768, 1536, value_width)
    halves = []
    half = model_width // 2
    core = where["core"]
    for color, order in enumerate(ORDERS):
        columns = value_grad[:, bounds[color] : bounds[color + 1]]
        last = color == len(ORDERS) - 1
        if last:
            spare = jnp.zeros((columns.shape[0], 128), columns.dtype)
            columns = jnp.concatenate([columns, spare], axis=1)
            gain_col = feature_order(gain_grad, order, seg_size, dp_size)
        ordered = feature_order(scaled, order, seg_size, dp_size)
        pair = []
        for pick in (core, 1 - core):
            rows = lax.dynamic_slice_in_dim(ordered, pick * half, half, 1)
            part = lax.dot_general(
                rows, columns, (((0,), (0,)), ((), ())), preferred_element_type=jnp.float32
            )
            if last:
                lane = lax.broadcasted_iota(jnp.int32, part.shape, 1)
                gain_half = lax.dynamic_slice_in_dim(gain_col, pick * half, half, 0)
                gain_lane = part.shape[1] - 128
                part = part + jnp.where(lane == gain_lane, gain_half[:, None], jnp.float32(0))
            pair.append(part)
        halves.append(pair)
    pieces = reduce_colours(halves, where)
    both = jnp.concatenate(pieces, axis=1)
    weight_part, gain_part = both[:, :value_width], both[:, value_width]
    return (hidden_grad.astype(jnp.bfloat16), summary_grad, weight_part, gain_part)


def solution(mesh):
    placed = (
        P("dp", "seg", None),
        P(),
        P(),
        P("dp", "seg", None),
        P("dp", "seg", None),
        P("dp", "seg", None),
        P("dp", "seg", None),
    )
    return jax.shard_map(
        local,
        mesh=mesh,
        in_specs=placed,
        out_specs=(
            P("dp", "seg", None),
            P("dp", "seg", None),
            P(("seg", "dp"), None),
            P(("seg", "dp")),
        ),
        check_vma=False,
    )
```

```python
import jax
import jax.numpy as jnp
from jax import lax
from jax.sharding import PartitionSpec as P

HEADS = 16
HEAD_DIM = 128


def passed_along(block, axis, distance):
    devices = range(lax.axis_size(axis))
    route = [(i - distance, i) for i in devices if i - distance in devices]
    return lax.ppermute(block, axis, route)


def mixing_of(query_rows, key_rows, summary_rows):
    trace_count, row_count, value_width = query_rows.shape
    slot_count = summary_rows.shape[1]
    query_heads = query_rows.reshape(trace_count, row_count, HEADS, HEAD_DIM)
    all_keys = jnp.concatenate([summary_rows, key_rows], axis=1)
    all_keys = all_keys.reshape(trace_count, slot_count + row_count, HEADS, HEAD_DIM)
    scores = jnp.einsum(
        "trhd,tkhd->thrk", query_heads, all_keys, preferred_element_type=jnp.float32
    )
    scores = scores * HEAD_DIM ** (-0.5)
    row_pos = lax.broadcasted_iota(jnp.int32, (row_count, slot_count + row_count), 0)
    col_pos = lax.broadcasted_iota(jnp.int32, (row_count, slot_count + row_count), 1)
    scores = jnp.where(col_pos <= row_pos + slot_count, scores, jnp.float32(-1e30))
    row_peak = jnp.max(scores, axis=-1, keepdims=True)
    exp_scores = jnp.exp(scores - row_peak)
    return (exp_scores / jnp.sum(exp_scores, axis=-1, keepdims=True)).astype(jnp.bfloat16)


def apply_map(matrix, state):
    return jnp.einsum("thkr,trhd->tkhd", matrix, state, precision=lax.Precision.HIGHEST)


def shifted(size, move):
    return [(i, move(i)) for i in range(size)]


def reduction_plan(seg_size, dp_size):
    x_n, z_n = seg_size // 4, dp_size // 2

    def y_move(sign):
        def move(i):
            s, d = divmod(i, dp_size)
            y = (2 * (d // z_n) + (s // 2) % 2 + sign) % 4
            return ((s // 4) * 4 + (y % 2) * 2 + s % 2) * dp_size + (y // 2) * z_n + d % z_n
        return move

    perms = {
        "x": [shifted(seg_size, lambda i, g=g: ((i // 4 + g) % x_n) * 4 + i % 4) for g in (1, -1, 2)],
        "z": [shifted(dp_size, lambda i, g=g: (i // z_n) * z_n + (i % z_n + g) % z_n) for g in (1, -1, 2)],
        "y": [shifted(seg_size * dp_size, y_move(g)) for g in (1, -1, 2)],
        "core": shifted(seg_size, lambda i: i ^ 1),
    }
    axes = {"x": "seg", "z": "dp", "y": ("seg", "dp")}
    return perms, axes


ORDERS = (("x", "y", "z"), ("y", "z", "x"), ("z", "y", "x"))


def feature_order(array, order, seg_size, dp_size):
    lead = array.shape[:-1]
    x_n, z_n = seg_size // 4, dp_size // 2
    split = array.reshape(*lead, x_n, 2, 2, 2, z_n, -1)
    n = len(lead)
    place = {"x": [n], "y": [n + 3, n + 1], "z": [n + 4], "core": [n + 2]}
    axes = list(range(n)) + place["core"] + [a for dim in order for a in place[dim]] + [n + 5]
    return split.transpose(axes).reshape(array.shape)


def ring_stage(parts, stage, where, perms, axes):
    groups = {}
    for color, order in enumerate(ORDERS):
        groups.setdefault(order[stage], []).append(color)
    dims = list(groups)
    split = []
    for members in groups.values():
        part = jnp.concatenate([parts[c] for c in members], axis=1)
        rows, cols = part.shape
        quarter = part.reshape(4, 2, rows // 8, cols)
        split.append((quarter[:, 0], quarter[:, 1]))

    def own(block, index):
        return lax.dynamic_index_in_dim(block, index % 4, 0, keepdims=False)

    acc = [
        (own(ahead, where[dim] - 1), own(behind, where[dim] + 1))
        for dim, (ahead, behind) in zip(dims, split)
    ]
    for step in (2, 3, 4):
        moved = [
            (lax.ppermute(a, axes[dim], perms[dim][0]), lax.ppermute(b, axes[dim], perms[dim][1]))
            for dim, (a, b) in zip(dims, acc)
        ]
        moved = lax.optimization_barrier(moved)
        acc = [
            (a + own(ahead, where[dim] - step), b + own(behind, where[dim] + step))
            for dim, (a, b), (ahead, behind) in zip(dims, moved, split)
        ]
    parts = list(parts)
    for members, pair in zip(groups.values(), acc):
        total = jnp.concatenate(pair, axis=0)
        edge = 0
        for c in members:
            width = parts[c].shape[1]
            parts[c] = total[:, edge : edge + width]
            edge += width
    return parts


def reduce_colours(halves, where):
    perms, axes = reduction_plan(lax.axis_size("seg"), lax.axis_size("dp"))
    parts = [keep + lax.ppermute(send, "seg", perms["core"]) for keep, send in halves]
    parts = ring_stage(parts, 0, where, perms, axes)
    parts = ring_stage(parts, 1, where, perms, axes)
    for stage in range(2, 3):
        groups = {}
        for color, order in enumerate(ORDERS):
            groups.setdefault(order[stage], []).append(color)
        moved = []
        for dim, members in groups.items():
            part = jnp.concatenate([parts[c] for c in members], axis=1)
            rows, cols = part.shape
            chunks = part.reshape(4, rows // 4, cols)

            def own(index, chunks=chunks):
                return lax.dynamic_index_in_dim(chunks, index % 4, 0, keepdims=False)

            coord = where[dim]
            sends = [
                lax.ppermute(own(coord + 1), axes[dim], perms[dim][0]),
                lax.ppermute(own(coord - 1), axes[dim], perms[dim][1]),
                lax.ppermute(own(coord + 2), axes[dim], perms[dim][2]),
            ]
            moved.append((own(coord), sends))
        moved = lax.optimization_barrier(moved)
        for members, (mine, sends) in zip(groups.values(), moved):
            total = mine + sends[0] + sends[1] + sends[2]
            edge = 0
            for c in members:
                width = parts[c].shape[1]
                parts[c] = total[:, edge : edge + width]
                edge += width
    return parts


def local(hidden, norm_gain, value_weight, queries, token_keys, summary_keys, output_grad):
    trace_count, row_count, value_width = queries.shape
    slot_count = summary_keys.shape[1]
    model_width = hidden.shape[2]
    mixing = mixing_of(queries, token_keys, summary_keys)
    grad_heads = output_grad.reshape(trace_count, row_count, HEADS, HEAD_DIM)
    direct = jnp.einsum("thrk,trhd->tkhd", mixing, grad_heads, preferred_element_type=jnp.float32)
    slot_mixing = mixing[:, :, row_count - slot_count :, :].astype(jnp.float32)
    own_map = jnp.swapaxes(slot_mixing[..., :slot_count], 2, 3)
    own_offset = direct[:, :slot_count]

    chain_map, chain_offset = own_map, own_offset
    offset, seg_size = 1, lax.axis_size("seg")
    while 2 * offset < seg_size:
        far_offset = passed_along(chain_offset, "seg", -offset)
        far_map = passed_along(chain_map, "seg", -offset)
        chain_offset = apply_map(chain_map, far_offset) + chain_offset
        chain_map = jnp.einsum(
            "thkm,thmr->thkr", chain_map, far_map, precision=lax.Precision.HIGHEST
        )
        offset *= 2
    past_half = passed_along(chain_offset, "seg", -offset)
    past_next_half = passed_along(chain_offset, "seg", -offset - 1)
    next_map = passed_along(chain_map, "seg", -1)
    next_offset = passed_along(chain_offset, "seg", -1)
    summary_state = apply_map(chain_map, past_half) + chain_offset
    incoming = apply_map(next_map, past_next_half) + next_offset
    summary_grad = summary_state.reshape(trace_count, slot_count, value_width)
    token_part = jnp.einsum(
        "thrk,trhd->tkhd", slot_mixing[..., slot_count:], incoming, precision=lax.Precision.HIGHEST
    )
    value_grad = (direct[:, slot_count:] + token_part).astype(jnp.bfloat16)
    value_grad = value_grad.reshape(trace_count * row_count, value_width)
    hidden_f = hidden.astype(jnp.float32)
    inv_rms = lax.rsqrt(jnp.mean(hidden_f * hidden_f, axis=-1, keepdims=True) + 1e-05)
    normed = hidden_f * inv_rms
    gain_f = norm_gain.astype(jnp.float32)
    scaled = (normed * gain_f).astype(jnp.bfloat16).reshape(trace_count * row_count, model_width)
    normalized_gradient = lax.dot_general(
        value_grad, value_weight, (((1,), (1,)), ((), ())), preferred_element_type=jnp.float32
    )
    normalized_gradient = normalized_gradient.reshape(trace_count, row_count, model_width)
    gain_grad = jnp.sum(
        (normalized_gradient * normed).reshape(trace_count * row_count, model_width), axis=0
    )
    scaled_grad = normalized_gradient * gain_f
    hidden_grad = inv_rms * (
        scaled_grad - normed * jnp.mean(scaled_grad * normed, axis=-1, keepdims=True)
    )
    seg_index, dp_index = lax.axis_index("seg"), lax.axis_index("dp")
    z_n = lax.axis_size("dp") // 2
    where = {
        "x": seg_index // 4,
        "y": 2 * (dp_index // z_n) + (seg_index // 2) % 2,
        "z": dp_index % z_n,
        "core": seg_index % 2,
    }
    seg_size, dp_size = lax.axis_size("seg"), lax.axis_size("dp")
    bounds = (0, 768, 1536, value_width)
    halves = []
    half = model_width // 2
    core = where["core"]
    for color, order in enumerate(ORDERS):
        columns = value_grad[:, bounds[color] : bounds[color + 1]]
        last = color == len(ORDERS) - 1
        if last:
            spare = jnp.zeros((columns.shape[0], 128), columns.dtype)
            columns = jnp.concatenate([columns, spare], axis=1)
            gain_col = feature_order(gain_grad, order, seg_size, dp_size)
        ordered = feature_order(scaled, order, seg_size, dp_size)
        pair = []
        for pick in (core, 1 - core):
            rows = lax.dynamic_slice_in_dim(ordered, pick * half, half, 1)
            part = lax.dot_general(
                rows, columns, (((0,), (0,)), ((), ())), preferred_element_type=jnp.float32
            )
            if last:
                lane = lax.broadcasted_iota(jnp.int32, part.shape, 1)
                gain_half = lax.dynamic_slice_in_dim(gain_col, pick * half, half, 0)
                gain_lane = part.shape[1] - 128
                part = part + jnp.where(lane == gain_lane, gain_half[:, None], jnp.float32(0))
            pair.append(part)
        halves.append(pair)
    pieces = reduce_colours(halves, where)
    both = jnp.concatenate(pieces, axis=1)
    weight_part, gain_part = both[:, :value_width], both[:, value_width]
    return (hidden_grad.astype(jnp.bfloat16), summary_grad, weight_part, gain_part)


def solution(mesh):
    placed = (
        P("dp", "seg", None),
        P(),
        P(),
        P("dp", "seg", None),
        P("dp", "seg", None),
        P("dp", "seg", None),
        P("dp", "seg", None),
    )
    return jax.shard_map(
        local,
        mesh=mesh,
        in_specs=placed,
        out_specs=(
            P("dp", "seg", None),
            P("dp", "seg", None),
            P(("seg", "dp"), None),
            P(("seg", "dp")),
        ),
        check_vma=False,
    )
```

```python
import jax
import jax.numpy as jnp
from jax import lax
from jax.sharding import PartitionSpec as P

HEADS = 16
HEAD_DIM = 128


def passed_along(block, axis, distance):
    devices = range(lax.axis_size(axis))
    route = [(i - distance, i) for i in devices if i - distance in devices]
    return lax.ppermute(block, axis, route)


def mixing_of(query_rows, key_rows, summary_rows):
    trace_count, row_count, value_width = query_rows.shape
    slot_count = summary_rows.shape[1]
    query_heads = query_rows.reshape(trace_count, row_count, HEADS, HEAD_DIM)
    all_keys = jnp.concatenate([summary_rows, key_rows], axis=1)
    all_keys = all_keys.reshape(trace_count, slot_count + row_count, HEADS, HEAD_DIM)
    scores = jnp.einsum(
        "trhd,tkhd->thrk", query_heads, all_keys, preferred_element_type=jnp.float32
    )
    scores = scores * HEAD_DIM ** (-0.5)
    row_pos = lax.broadcasted_iota(jnp.int32, (row_count, slot_count + row_count), 0)
    col_pos = lax.broadcasted_iota(jnp.int32, (row_count, slot_count + row_count), 1)
    scores = jnp.where(col_pos <= row_pos + slot_count, scores, jnp.float32(-1e30))
    row_peak = jnp.max(scores, axis=-1, keepdims=True)
    exp_scores = jnp.exp(scores - row_peak)
    return (exp_scores / jnp.sum(exp_scores, axis=-1, keepdims=True)).astype(jnp.bfloat16)


def apply_map(matrix, state):
    return jnp.einsum("thkr,trhd->tkhd", matrix, state, precision=lax.Precision.HIGHEST)


def shifted(size, move):
    return [(i, move(i)) for i in range(size)]


def reduction_plan(seg_size, dp_size):
    x_n, z_n = seg_size // 4, dp_size // 2

    def y_move(sign):
        def move(i):
            s, d = divmod(i, dp_size)
            y = (2 * (d // z_n) + (s // 2) % 2 + sign) % 4
            return ((s // 4) * 4 + (y % 2) * 2 + s % 2) * dp_size + (y // 2) * z_n + d % z_n
        return move

    perms = {
        "x": [shifted(seg_size, lambda i, g=g: ((i // 4 + g) % x_n) * 4 + i % 4) for g in (1, -1, 2)],
        "z": [shifted(dp_size, lambda i, g=g: (i // z_n) * z_n + (i % z_n + g) % z_n) for g in (1, -1, 2)],
        "y": [shifted(seg_size * dp_size, y_move(g)) for g in (1, -1, 2)],
        "core": shifted(seg_size, lambda i: i ^ 1),
    }
    axes = {"x": "seg", "z": "dp", "y": ("seg", "dp")}
    return perms, axes


ORDERS = (("x", "y", "z"), ("y", "z", "x"), ("z", "y", "x"))


def feature_order(array, order, seg_size, dp_size):
    lead = array.shape[:-1]
    x_n, z_n = seg_size // 4, dp_size // 2
    split = array.reshape(*lead, x_n, 2, 2, 2, z_n, -1)
    n = len(lead)
    place = {"x": [n], "y": [n + 3, n + 1], "z": [n + 4], "core": [n + 2]}
    axes = list(range(n)) + place["core"] + [a for dim in order for a in place[dim]] + [n + 5]
    return split.transpose(axes).reshape(array.shape)


def ring_first_stage(parts, where, perms, axes):
    dims = [order[0] for order in ORDERS]
    split = []
    for part in parts:
        rows, cols = part.shape
        quarter = part.reshape(4, 2, rows // 8, cols)
        split.append((quarter[:, 0], quarter[:, 1]))

    def own(block, index):
        return lax.dynamic_index_in_dim(block, index % 4, 0, keepdims=False)

    acc = [
        (own(ahead, where[dim] - 1), own(behind, where[dim] + 1))
        for dim, (ahead, behind) in zip(dims, split)
    ]
    for step in (2, 3, 4):
        acc = lax.optimization_barrier(acc)
        moved = [
            (lax.ppermute(a, axes[dim], perms[dim][0]), lax.ppermute(b, axes[dim], perms[dim][1]))
            for dim, (a, b) in zip(dims, acc)
        ]
        acc = [
            (a + own(ahead, where[dim] - step), b + own(behind, where[dim] + step))
            for dim, (a, b), (ahead, behind) in zip(dims, moved, split)
        ]
    return [jnp.concatenate(pair, axis=0) for pair in acc]


def reduce_colours(halves, where):
    perms, axes = reduction_plan(lax.axis_size("seg"), lax.axis_size("dp"))
    parts = [keep + lax.ppermute(send, "seg", perms["core"]) for keep, send in halves]
    parts = ring_first_stage(parts, where, perms, axes)
    for stage in range(1, 3):
        groups = {}
        for color, order in enumerate(ORDERS):
            groups.setdefault(order[stage], []).append(color)
        moved = []
        for dim, members in groups.items():
            part = jnp.concatenate([parts[c] for c in members], axis=1)
            rows, cols = part.shape
            chunks = part.reshape(4, rows // 4, cols)

            def own(index, chunks=chunks):
                return lax.dynamic_index_in_dim(chunks, index % 4, 0, keepdims=False)

            coord = where[dim]
            sends = [
                lax.ppermute(own(coord + 1), axes[dim], perms[dim][0]),
                lax.ppermute(own(coord - 1), axes[dim], perms[dim][1]),
                lax.ppermute(own(coord + 2), axes[dim], perms[dim][2]),
            ]
            moved.append((own(coord), sends))
        moved = lax.optimization_barrier(moved)
        for members, (mine, sends) in zip(groups.values(), moved):
            total = mine + sends[0] + sends[1] + sends[2]
            edge = 0
            for c in members:
                width = parts[c].shape[1]
                parts[c] = total[:, edge : edge + width]
                edge += width
    return parts


def local(hidden, norm_gain, value_weight, queries, token_keys, summary_keys, output_grad):
    trace_count, row_count, value_width = queries.shape
    slot_count = summary_keys.shape[1]
    model_width = hidden.shape[2]
    mixing = mixing_of(queries, token_keys, summary_keys)
    grad_heads = output_grad.reshape(trace_count, row_count, HEADS, HEAD_DIM)
    direct = jnp.einsum("thrk,trhd->tkhd", mixing, grad_heads, preferred_element_type=jnp.float32)
    slot_mixing = mixing[:, :, row_count - slot_count :, :].astype(jnp.float32)
    own_map = jnp.swapaxes(slot_mixing[..., :slot_count], 2, 3)
    own_offset = direct[:, :slot_count]

    chain_map, chain_offset = own_map, own_offset
    offset, seg_size = 1, lax.axis_size("seg")
    while 2 * offset < seg_size:
        far_offset = passed_along(chain_offset, "seg", -offset)
        far_map = passed_along(chain_map, "seg", -offset)
        chain_offset = apply_map(chain_map, far_offset) + chain_offset
        chain_map = jnp.einsum(
            "thkm,thmr->thkr", chain_map, far_map, precision=lax.Precision.HIGHEST
        )
        offset *= 2
    past_half = passed_along(chain_offset, "seg", -offset)
    past_next_half = passed_along(chain_offset, "seg", -offset - 1)
    next_map = passed_along(chain_map, "seg", -1)
    next_offset = passed_along(chain_offset, "seg", -1)
    summary_state = apply_map(chain_map, past_half) + chain_offset
    incoming = apply_map(next_map, past_next_half) + next_offset
    summary_grad = summary_state.reshape(trace_count, slot_count, value_width)
    token_part = jnp.einsum(
        "thrk,trhd->tkhd", slot_mixing[..., slot_count:], incoming, precision=lax.Precision.HIGHEST
    )
    value_grad = (direct[:, slot_count:] + token_part).astype(jnp.bfloat16)
    value_grad = value_grad.reshape(trace_count * row_count, value_width)
    hidden_f = hidden.astype(jnp.float32)
    inv_rms = lax.rsqrt(jnp.mean(hidden_f * hidden_f, axis=-1, keepdims=True) + 1e-05)
    normed = hidden_f * inv_rms
    gain_f = norm_gain.astype(jnp.float32)
    scaled = (normed * gain_f).astype(jnp.bfloat16).reshape(trace_count * row_count, model_width)
    normalized_gradient = lax.dot_general(
        value_grad, value_weight, (((1,), (1,)), ((), ())), preferred_element_type=jnp.float32
    )
    normalized_gradient = normalized_gradient.reshape(trace_count, row_count, model_width)
    gain_grad = jnp.sum(
        (normalized_gradient * normed).reshape(trace_count * row_count, model_width), axis=0
    )
    scaled_grad = normalized_gradient * gain_f
    hidden_grad = inv_rms * (
        scaled_grad - normed * jnp.mean(scaled_grad * normed, axis=-1, keepdims=True)
    )
    seg_index, dp_index = lax.axis_index("seg"), lax.axis_index("dp")
    z_n = lax.axis_size("dp") // 2
    where = {
        "x": seg_index // 4,
        "y": 2 * (dp_index // z_n) + (seg_index // 2) % 2,
        "z": dp_index % z_n,
        "core": seg_index % 2,
    }
    seg_size, dp_size = lax.axis_size("seg"), lax.axis_size("dp")
    bounds = (0, 768, 1536, value_width)
    halves = []
    half = model_width // 2
    core = where["core"]
    for color, order in enumerate(ORDERS):
        columns = value_grad[:, bounds[color] : bounds[color + 1]]
        last = color == len(ORDERS) - 1
        if last:
            spare = jnp.zeros((columns.shape[0], 128), columns.dtype)
            columns = jnp.concatenate([columns, spare], axis=1)
            gain_col = feature_order(gain_grad, order, seg_size, dp_size)
        ordered = feature_order(scaled, order, seg_size, dp_size)
        pair = []
        for pick in (core, 1 - core):
            rows = lax.dynamic_slice_in_dim(ordered, pick * half, half, 1)
            part = lax.dot_general(
                rows, columns, (((0,), (0,)), ((), ())), preferred_element_type=jnp.float32
            )
            if last:
                lane = lax.broadcasted_iota(jnp.int32, part.shape, 1)
                gain_half = lax.dynamic_slice_in_dim(gain_col, pick * half, half, 0)
                gain_lane = part.shape[1] - 128
                part = part + jnp.where(lane == gain_lane, gain_half[:, None], jnp.float32(0))
            pair.append(part)
        halves.append(pair)
    pieces = reduce_colours(halves, where)
    both = jnp.concatenate(pieces, axis=1)
    weight_part, gain_part = both[:, :value_width], both[:, value_width]
    return (hidden_grad.astype(jnp.bfloat16), summary_grad, weight_part, gain_part)


def solution(mesh):
    placed = (
        P("dp", "seg", None),
        P(),
        P(),
        P("dp", "seg", None),
        P("dp", "seg", None),
        P("dp", "seg", None),
        P("dp", "seg", None),
    )
    return jax.shard_map(
        local,
        mesh=mesh,
        in_specs=placed,
        out_specs=(
            P("dp", "seg", None),
            P("dp", "seg", None),
            P(("seg", "dp"), None),
            P(("seg", "dp")),
        ),
        check_vma=False,
    )
```

```python
import jax
import jax.numpy as jnp
from jax import lax
from jax.sharding import PartitionSpec as P

HEADS = 16
HEAD_DIM = 128


def passed_along(block, axis, distance):
    devices = range(lax.axis_size(axis))
    route = [(i - distance, i) for i in devices if i - distance in devices]
    return lax.ppermute(block, axis, route)


def mixing_of(query_rows, key_rows, summary_rows):
    trace_count, row_count, value_width = query_rows.shape
    slot_count = summary_rows.shape[1]
    query_heads = query_rows.reshape(trace_count, row_count, HEADS, HEAD_DIM)
    all_keys = jnp.concatenate([summary_rows, key_rows], axis=1)
    all_keys = all_keys.reshape(trace_count, slot_count + row_count, HEADS, HEAD_DIM)
    scores = jnp.einsum(
        "trhd,tkhd->thrk", query_heads, all_keys, preferred_element_type=jnp.float32
    )
    scores = scores * HEAD_DIM ** (-0.5)
    row_pos = lax.broadcasted_iota(jnp.int32, (row_count, slot_count + row_count), 0)
    col_pos = lax.broadcasted_iota(jnp.int32, (row_count, slot_count + row_count), 1)
    scores = jnp.where(col_pos <= row_pos + slot_count, scores, jnp.float32(-1e30))
    row_peak = jnp.max(scores, axis=-1, keepdims=True)
    exp_scores = jnp.exp(scores - row_peak)
    return (exp_scores / jnp.sum(exp_scores, axis=-1, keepdims=True)).astype(jnp.bfloat16)


def apply_map(matrix, state):
    return jnp.einsum("thkr,trhd->tkhd", matrix, state, precision=lax.Precision.HIGHEST)


def shifted(size, move):
    return [(i, move(i)) for i in range(size)]


def reduction_plan(seg_size, dp_size):
    x_n, z_n = seg_size // 4, dp_size // 2

    def y_move(sign):
        def move(i):
            s, d = divmod(i, dp_size)
            y = (2 * (d // z_n) + (s // 2) % 2 + sign) % 4
            return ((s // 4) * 4 + (y % 2) * 2 + s % 2) * dp_size + (y // 2) * z_n + d % z_n
        return move

    perms = {
        "x": [shifted(seg_size, lambda i, g=g: ((i // 4 + g) % x_n) * 4 + i % 4) for g in (1, -1, 2)],
        "z": [shifted(dp_size, lambda i, g=g: (i // z_n) * z_n + (i % z_n + g) % z_n) for g in (1, -1, 2)],
        "y": [shifted(seg_size * dp_size, y_move(g)) for g in (1, -1, 2)],
        "core": shifted(seg_size, lambda i: i ^ 1),
    }
    axes = {"x": "seg", "z": "dp", "y": ("seg", "dp")}
    return perms, axes


ORDERS = (("x", "y", "z"), ("y", "z", "x"), ("z", "y", "x"))


def feature_order(array, order, seg_size, dp_size):
    lead = array.shape[:-1]
    x_n, z_n = seg_size // 4, dp_size // 2
    split = array.reshape(*lead, x_n, 2, 2, 2, z_n, -1)
    n = len(lead)
    place = {"x": [n], "y": [n + 3, n + 1], "z": [n + 4], "core": [n + 2]}
    axes = list(range(n)) + place["core"] + [a for dim in order for a in place[dim]] + [n + 5]
    return split.transpose(axes).reshape(array.shape)


def ring_first_stage(parts, where, perms, axes):
    dims = [order[0] for order in ORDERS]
    split = []
    for part in parts:
        rows, cols = part.shape
        quarter = part.reshape(4, 2, rows // 8, cols)
        split.append((quarter[:, 0], quarter[:, 1]))

    def own(block, index):
        return lax.dynamic_index_in_dim(block, index % 4, 0, keepdims=False)

    acc = [
        (own(ahead, where[dim] - 1), own(behind, where[dim] + 1))
        for dim, (ahead, behind) in zip(dims, split)
    ]
    for step in (2, 3, 4):
        moved = [
            (lax.ppermute(a, axes[dim], perms[dim][0]), lax.ppermute(b, axes[dim], perms[dim][1]))
            for dim, (a, b) in zip(dims, acc)
        ]
        moved = lax.optimization_barrier(moved)
        acc = [
            (a + own(ahead, where[dim] - step), b + own(behind, where[dim] + step))
            for dim, (a, b), (ahead, behind) in zip(dims, moved, split)
        ]
    return [jnp.concatenate(pair, axis=0) for pair in acc]


def reduce_colours(halves, where):
    perms, axes = reduction_plan(lax.axis_size("seg"), lax.axis_size("dp"))
    parts = [keep + lax.ppermute(send, "seg", perms["core"]) for keep, send in halves]
    parts = ring_first_stage(parts, where, perms, axes)
    for stage in range(1, 3):
        groups = {}
        for color, order in enumerate(ORDERS):
            groups.setdefault(order[stage], []).append(color)
        moved = []
        for dim, members in groups.items():
            part = jnp.concatenate([parts[c] for c in members], axis=1)
            rows, cols = part.shape
            chunks = part.reshape(4, rows // 4, cols)

            def own(index, chunks=chunks):
                return lax.dynamic_index_in_dim(chunks, index % 4, 0, keepdims=False)

            coord = where[dim]
            sends = [
                lax.ppermute(own(coord + 1), axes[dim], perms[dim][0]),
                lax.ppermute(own(coord - 1), axes[dim], perms[dim][1]),
                lax.ppermute(own(coord + 2), axes[dim], perms[dim][2]),
            ]
            moved.append((own(coord), sends))
        moved = lax.optimization_barrier(moved)
        for members, (mine, sends) in zip(groups.values(), moved):
            total = mine + sends[0] + sends[1] + sends[2]
            edge = 0
            for c in members:
                width = parts[c].shape[1]
                parts[c] = total[:, edge : edge + width]
                edge += width
    return parts


def local(hidden, norm_gain, value_weight, queries, token_keys, summary_keys, output_grad):
    trace_count, row_count, value_width = queries.shape
    slot_count = summary_keys.shape[1]
    model_width = hidden.shape[2]
    mixing = mixing_of(queries, token_keys, summary_keys)
    grad_heads = output_grad.reshape(trace_count, row_count, HEADS, HEAD_DIM)
    direct = jnp.einsum("thrk,trhd->tkhd", mixing, grad_heads, preferred_element_type=jnp.float32)
    slot_mixing = mixing[:, :, row_count - slot_count :, :].astype(jnp.float32)
    own_map = jnp.swapaxes(slot_mixing[..., :slot_count], 2, 3)
    own_offset = direct[:, :slot_count]

    chain_map, chain_offset = own_map, own_offset
    offset, seg_size = 1, lax.axis_size("seg")
    assert seg_size == 16
    far_offset = passed_along(chain_offset, "seg", -offset)
    far_map = passed_along(chain_map, "seg", -offset)
    chain_offset = apply_map(chain_map, far_offset) + chain_offset
    chain_map = jnp.einsum("thkm,thmr->thkr", chain_map, far_map, precision=lax.Precision.HIGHEST)
    offset = 2
    far = [
        (passed_along(chain_map, "seg", -k * offset), passed_along(chain_offset, "seg", -k * offset))
        for k in (1, 2, 3)
    ]
    acc_map, acc_offset = far[2]
    for near_map, near_offset in (far[1], far[0]):
        acc_offset = apply_map(near_map, acc_offset) + near_offset
        acc_map = jnp.einsum("thkm,thmr->thkr", near_map, acc_map, precision=lax.Precision.HIGHEST)
    chain_offset = apply_map(chain_map, acc_offset) + chain_offset
    chain_map = jnp.einsum("thkm,thmr->thkr", chain_map, acc_map, precision=lax.Precision.HIGHEST)
    offset = 8
    past_half = passed_along(chain_offset, "seg", -offset)
    past_next_half = passed_along(chain_offset, "seg", -offset - 1)
    next_map = passed_along(chain_map, "seg", -1)
    next_offset = passed_along(chain_offset, "seg", -1)
    summary_state = apply_map(chain_map, past_half) + chain_offset
    incoming = apply_map(next_map, past_next_half) + next_offset
    summary_grad = summary_state.reshape(trace_count, slot_count, value_width)
    token_part = jnp.einsum(
        "thrk,trhd->tkhd", slot_mixing[..., slot_count:], incoming, precision=lax.Precision.HIGHEST
    )
    value_grad = (direct[:, slot_count:] + token_part).astype(jnp.bfloat16)
    value_grad = value_grad.reshape(trace_count * row_count, value_width)
    hidden_f = hidden.astype(jnp.float32)
    inv_rms = lax.rsqrt(jnp.mean(hidden_f * hidden_f, axis=-1, keepdims=True) + 1e-05)
    normed = hidden_f * inv_rms
    gain_f = norm_gain.astype(jnp.float32)
    scaled = (normed * gain_f).astype(jnp.bfloat16).reshape(trace_count * row_count, model_width)
    normalized_gradient = lax.dot_general(
        value_grad, value_weight, (((1,), (1,)), ((), ())), preferred_element_type=jnp.float32
    )
    normalized_gradient = normalized_gradient.reshape(trace_count, row_count, model_width)
    gain_grad = jnp.sum(
        (normalized_gradient * normed).reshape(trace_count * row_count, model_width), axis=0
    )
    scaled_grad = normalized_gradient * gain_f
    hidden_grad = inv_rms * (
        scaled_grad - normed * jnp.mean(scaled_grad * normed, axis=-1, keepdims=True)
    )
    seg_index, dp_index = lax.axis_index("seg"), lax.axis_index("dp")
    z_n = lax.axis_size("dp") // 2
    where = {
        "x": seg_index // 4,
        "y": 2 * (dp_index // z_n) + (seg_index // 2) % 2,
        "z": dp_index % z_n,
        "core": seg_index % 2,
    }
    seg_size, dp_size = lax.axis_size("seg"), lax.axis_size("dp")
    bounds = (0, 768, 1536, value_width)
    halves = []
    half = model_width // 2
    core = where["core"]
    for color, order in enumerate(ORDERS):
        columns = value_grad[:, bounds[color] : bounds[color + 1]]
        last = color == len(ORDERS) - 1
        if last:
            spare = jnp.zeros((columns.shape[0], 128), columns.dtype)
            columns = jnp.concatenate([columns, spare], axis=1)
            gain_col = feature_order(gain_grad, order, seg_size, dp_size)
        ordered = feature_order(scaled, order, seg_size, dp_size)
        pair = []
        for pick in (core, 1 - core):
            rows = lax.dynamic_slice_in_dim(ordered, pick * half, half, 1)
            part = lax.dot_general(
                rows, columns, (((0,), (0,)), ((), ())), preferred_element_type=jnp.float32
            )
            if last:
                lane = lax.broadcasted_iota(jnp.int32, part.shape, 1)
                gain_half = lax.dynamic_slice_in_dim(gain_col, pick * half, half, 0)
                gain_lane = part.shape[1] - 128
                part = part + jnp.where(lane == gain_lane, gain_half[:, None], jnp.float32(0))
            pair.append(part)
        halves.append(pair)
    pieces = reduce_colours(halves, where)
    both = jnp.concatenate(pieces, axis=1)
    weight_part, gain_part = both[:, :value_width], both[:, value_width]
    return (hidden_grad.astype(jnp.bfloat16), summary_grad, weight_part, gain_part)


def solution(mesh):
    placed = (
        P("dp", "seg", None),
        P(),
        P(),
        P("dp", "seg", None),
        P("dp", "seg", None),
        P("dp", "seg", None),
        P("dp", "seg", None),
    )
    return jax.shard_map(
        local,
        mesh=mesh,
        in_specs=placed,
        out_specs=(
            P("dp", "seg", None),
            P("dp", "seg", None),
            P(("seg", "dp"), None),
            P(("seg", "dp")),
        ),
        check_vma=False,
    )
```

```python
import jax
import jax.numpy as jnp
from jax import lax
from jax.sharding import PartitionSpec as P

HEADS = 16
HEAD_DIM = 128


def passed_along(block, axis, distance):
    devices = range(lax.axis_size(axis))
    route = [(i - distance, i) for i in devices if i - distance in devices]
    return lax.ppermute(block, axis, route)


def mixing_of(query_rows, key_rows, summary_rows):
    trace_count, row_count, value_width = query_rows.shape
    slot_count = summary_rows.shape[1]
    query_heads = query_rows.reshape(trace_count, row_count, HEADS, HEAD_DIM)
    all_keys = jnp.concatenate([summary_rows, key_rows], axis=1)
    all_keys = all_keys.reshape(trace_count, slot_count + row_count, HEADS, HEAD_DIM)
    scores = jnp.einsum(
        "trhd,tkhd->thrk", query_heads, all_keys, preferred_element_type=jnp.float32
    )
    scores = scores * HEAD_DIM ** (-0.5)
    row_pos = lax.broadcasted_iota(jnp.int32, (row_count, slot_count + row_count), 0)
    col_pos = lax.broadcasted_iota(jnp.int32, (row_count, slot_count + row_count), 1)
    scores = jnp.where(col_pos <= row_pos + slot_count, scores, jnp.float32(-1e30))
    row_peak = jnp.max(scores, axis=-1, keepdims=True)
    exp_scores = jnp.exp(scores - row_peak)
    return (exp_scores / jnp.sum(exp_scores, axis=-1, keepdims=True)).astype(jnp.bfloat16)


def apply_map(matrix, state):
    return jnp.einsum("thkr,trhd->tkhd", matrix, state, precision=lax.Precision.HIGHEST)


def shifted(size, move):
    return [(i, move(i)) for i in range(size)]


def reduction_plan(seg_size, dp_size):
    x_n, z_n = seg_size // 4, dp_size // 2

    def y_move(sign):
        def move(i):
            s, d = divmod(i, dp_size)
            y = (2 * (d // z_n) + (s // 2) % 2 + sign) % 4
            return ((s // 4) * 4 + (y % 2) * 2 + s % 2) * dp_size + (y // 2) * z_n + d % z_n
        return move

    perms = {
        "x": [shifted(seg_size, lambda i, g=g: ((i // 4 + g) % x_n) * 4 + i % 4) for g in (1, -1, 2)],
        "z": [shifted(dp_size, lambda i, g=g: (i // z_n) * z_n + (i % z_n + g) % z_n) for g in (1, -1, 2)],
        "y": [shifted(seg_size * dp_size, y_move(g)) for g in (1, -1, 2)],
        "core": shifted(seg_size, lambda i: i ^ 1),
    }
    axes = {"x": "seg", "z": "dp", "y": ("seg", "dp")}
    return perms, axes


ORDERS = (("x", "y", "z"), ("y", "z", "x"), ("z", "y", "x"))


def feature_order(array, order, seg_size, dp_size):
    lead = array.shape[:-1]
    x_n, z_n = seg_size // 4, dp_size // 2
    split = array.reshape(*lead, x_n, 2, 2, 2, z_n, -1)
    n = len(lead)
    place = {"x": [n], "y": [n + 3, n + 1], "z": [n + 4], "core": [n + 2]}
    axes = list(range(n)) + place["core"] + [a for dim in order for a in place[dim]] + [n + 5]
    return split.transpose(axes).reshape(array.shape)


def ring_first_stage(parts, where, perms, axes):
    dims = [order[0] for order in ORDERS]
    split = []
    for part in parts:
        rows, cols = part.shape
        quarter = part.reshape(4, 2, rows // 8, cols)
        split.append((quarter[:, 0], quarter[:, 1]))

    def own(block, index):
        return lax.dynamic_index_in_dim(block, index % 4, 0, keepdims=False)

    acc = [
        (own(ahead, where[dim] - 1), own(behind, where[dim] + 1))
        for dim, (ahead, behind) in zip(dims, split)
    ]
    for step in (2, 3, 4):
        moved = [
            (lax.ppermute(a, axes[dim], perms[dim][0]), lax.ppermute(b, axes[dim], perms[dim][1]))
            for dim, (a, b) in zip(dims, acc)
        ]
        moved = lax.optimization_barrier(moved)
        acc = [
            (a + own(ahead, where[dim] - step), b + own(behind, where[dim] + step))
            for dim, (a, b), (ahead, behind) in zip(dims, moved, split)
        ]
    return [jnp.concatenate(pair, axis=0) for pair in acc]


def reduce_colours(halves, where):
    perms, axes = reduction_plan(lax.axis_size("seg"), lax.axis_size("dp"))
    parts = [keep + lax.ppermute(send, "seg", perms["core"]) for keep, send in halves]
    parts = ring_first_stage(parts, where, perms, axes)
    for stage in range(1, 3):
        groups = {}
        for color, order in enumerate(ORDERS):
            groups.setdefault(order[stage], []).append(color)
        moved = []
        for dim, members in groups.items():
            part = jnp.concatenate([parts[c] for c in members], axis=1)
            rows, cols = part.shape
            chunks = part.reshape(4, rows // 4, cols)

            def own(index, chunks=chunks):
                return lax.dynamic_index_in_dim(chunks, index % 4, 0, keepdims=False)

            coord = where[dim]
            sends = [
                lax.ppermute(own(coord + 1), axes[dim], perms[dim][0]),
                lax.ppermute(own(coord - 1), axes[dim], perms[dim][1]),
                lax.ppermute(own(coord + 2), axes[dim], perms[dim][2]),
            ]
            moved.append((own(coord), sends))
        for members, (mine, sends) in zip(groups.values(), moved):
            total = mine + sends[0] + sends[1] + sends[2]
            edge = 0
            for c in members:
                width = parts[c].shape[1]
                parts[c] = total[:, edge : edge + width]
                edge += width
    return parts


def local(hidden, norm_gain, value_weight, queries, token_keys, summary_keys, output_grad):
    trace_count, row_count, value_width = queries.shape
    slot_count = summary_keys.shape[1]
    model_width = hidden.shape[2]
    mixing = mixing_of(queries, token_keys, summary_keys)
    grad_heads = output_grad.reshape(trace_count, row_count, HEADS, HEAD_DIM)
    direct = jnp.einsum("thrk,trhd->tkhd", mixing, grad_heads, preferred_element_type=jnp.float32)
    slot_mixing = mixing[:, :, row_count - slot_count :, :].astype(jnp.float32)
    own_map = jnp.swapaxes(slot_mixing[..., :slot_count], 2, 3)
    own_offset = direct[:, :slot_count]

    chain_map, chain_offset = own_map, own_offset
    offset, seg_size = 1, lax.axis_size("seg")
    while 2 * offset < seg_size:
        far_offset = passed_along(chain_offset, "seg", -offset)
        far_map = passed_along(chain_map, "seg", -offset)
        chain_offset = apply_map(chain_map, far_offset) + chain_offset
        chain_map = jnp.einsum(
            "thkm,thmr->thkr", chain_map, far_map, precision=lax.Precision.HIGHEST
        )
        offset *= 2
    past_half = passed_along(chain_offset, "seg", -offset)
    past_next_half = passed_along(chain_offset, "seg", -offset - 1)
    next_map = passed_along(chain_map, "seg", -1)
    next_offset = passed_along(chain_offset, "seg", -1)
    summary_state = apply_map(chain_map, past_half) + chain_offset
    incoming = apply_map(next_map, past_next_half) + next_offset
    summary_grad = summary_state.reshape(trace_count, slot_count, value_width)
    token_part = jnp.einsum(
        "thrk,trhd->tkhd", slot_mixing[..., slot_count:], incoming, precision=lax.Precision.HIGHEST
    )
    value_grad = (direct[:, slot_count:] + token_part).astype(jnp.bfloat16)
    value_grad = value_grad.reshape(trace_count * row_count, value_width)
    hidden_f = hidden.astype(jnp.float32)
    inv_rms = lax.rsqrt(jnp.mean(hidden_f * hidden_f, axis=-1, keepdims=True) + 1e-05)
    normed = hidden_f * inv_rms
    gain_f = norm_gain.astype(jnp.float32)
    scaled = (normed * gain_f).astype(jnp.bfloat16).reshape(trace_count * row_count, model_width)
    normalized_gradient = lax.dot_general(
        value_grad, value_weight, (((1,), (1,)), ((), ())), preferred_element_type=jnp.float32
    )
    normalized_gradient = normalized_gradient.reshape(trace_count, row_count, model_width)
    gain_grad = jnp.sum(
        (normalized_gradient * normed).reshape(trace_count * row_count, model_width), axis=0
    )
    scaled_grad = normalized_gradient * gain_f
    hidden_grad = inv_rms * (
        scaled_grad - normed * jnp.mean(scaled_grad * normed, axis=-1, keepdims=True)
    )
    seg_index, dp_index = lax.axis_index("seg"), lax.axis_index("dp")
    z_n = lax.axis_size("dp") // 2
    where = {
        "x": seg_index // 4,
        "y": 2 * (dp_index // z_n) + (seg_index // 2) % 2,
        "z": dp_index % z_n,
        "core": seg_index % 2,
    }
    seg_size, dp_size = lax.axis_size("seg"), lax.axis_size("dp")
    bounds = (0, 768, 1536, value_width)
    halves = []
    half = model_width // 2
    core = where["core"]
    for color, order in enumerate(ORDERS):
        columns = value_grad[:, bounds[color] : bounds[color + 1]]
        last = color == len(ORDERS) - 1
        if last:
            spare = jnp.zeros((columns.shape[0], 128), columns.dtype)
            columns = jnp.concatenate([columns, spare], axis=1)
            gain_col = feature_order(gain_grad, order, seg_size, dp_size)
        ordered = feature_order(scaled, order, seg_size, dp_size)
        pair = []
        for pick in (core, 1 - core):
            rows = lax.dynamic_slice_in_dim(ordered, pick * half, half, 1)
            part = lax.dot_general(
                rows, columns, (((0,), (0,)), ((), ())), preferred_element_type=jnp.float32
            )
            if last:
                lane = lax.broadcasted_iota(jnp.int32, part.shape, 1)
                gain_half = lax.dynamic_slice_in_dim(gain_col, pick * half, half, 0)
                gain_lane = part.shape[1] - 128
                part = part + jnp.where(lane == gain_lane, gain_half[:, None], jnp.float32(0))
            pair.append(part)
        halves.append(pair)
    pieces = reduce_colours(halves, where)
    both = jnp.concatenate(pieces, axis=1)
    weight_part, gain_part = both[:, :value_width], both[:, value_width]
    return (hidden_grad.astype(jnp.bfloat16), summary_grad, weight_part, gain_part)


def solution(mesh):
    placed = (
        P("dp", "seg", None),
        P(),
        P(),
        P("dp", "seg", None),
        P("dp", "seg", None),
        P("dp", "seg", None),
        P("dp", "seg", None),
    )
    return jax.shard_map(
        local,
        mesh=mesh,
        in_specs=placed,
        out_specs=(
            P("dp", "seg", None),
            P("dp", "seg", None),
            P(("seg", "dp"), None),
            P(("seg", "dp")),
        ),
        check_vma=False,
    )
```

```python
import jax
import jax.numpy as jnp
from jax import lax
from jax.sharding import PartitionSpec as P

HEADS = 16
HEAD_DIM = 128


def passed_along(block, axis, distance):
    devices = range(lax.axis_size(axis))
    route = [(i - distance, i) for i in devices if i - distance in devices]
    return lax.ppermute(block, axis, route)


def mixing_of(query_rows, key_rows, summary_rows):
    trace_count, row_count, value_width = query_rows.shape
    slot_count = summary_rows.shape[1]
    query_heads = query_rows.reshape(trace_count, row_count, HEADS, HEAD_DIM)
    all_keys = jnp.concatenate([summary_rows, key_rows], axis=1)
    all_keys = all_keys.reshape(trace_count, slot_count + row_count, HEADS, HEAD_DIM)
    scores = jnp.einsum(
        "trhd,tkhd->thrk", query_heads, all_keys, preferred_element_type=jnp.float32
    )
    scores = scores * HEAD_DIM ** (-0.5)
    row_pos = lax.broadcasted_iota(jnp.int32, (row_count, slot_count + row_count), 0)
    col_pos = lax.broadcasted_iota(jnp.int32, (row_count, slot_count + row_count), 1)
    scores = jnp.where(col_pos <= row_pos + slot_count, scores, jnp.float32(-1e30))
    row_peak = jnp.max(scores, axis=-1, keepdims=True)
    exp_scores = jnp.exp(scores - row_peak)
    return (exp_scores / jnp.sum(exp_scores, axis=-1, keepdims=True)).astype(jnp.bfloat16)


def apply_map(matrix, state):
    return jnp.einsum("thkr,trhd->tkhd", matrix, state, precision=lax.Precision.HIGHEST)


def shifted(size, move):
    return [(i, move(i)) for i in range(size)]


def reduction_plan(seg_size, dp_size):
    x_n, z_n = seg_size // 4, dp_size // 2

    def y_move(sign):
        def move(i):
            s, d = divmod(i, dp_size)
            y = (2 * (d // z_n) + (s // 2) % 2 + sign) % 4
            return ((s // 4) * 4 + (y % 2) * 2 + s % 2) * dp_size + (y // 2) * z_n + d % z_n
        return move

    perms = {
        "x": [shifted(seg_size, lambda i, g=g: ((i // 4 + g) % x_n) * 4 + i % 4) for g in (1, -1, 2)],
        "z": [shifted(dp_size, lambda i, g=g: (i // z_n) * z_n + (i % z_n + g) % z_n) for g in (1, -1, 2)],
        "y": [shifted(seg_size * dp_size, y_move(g)) for g in (1, -1, 2)],
        "core": shifted(seg_size, lambda i: i ^ 1),
    }
    axes = {"x": "seg", "z": "dp", "y": ("seg", "dp")}
    return perms, axes


ORDERS = (("x", "y", "z"), ("y", "z", "x"), ("z", "y", "x"))


def feature_order(array, order, seg_size, dp_size):
    lead = array.shape[:-1]
    x_n, z_n = seg_size // 4, dp_size // 2
    split = array.reshape(*lead, x_n, 2, 2, 2, z_n, -1)
    n = len(lead)
    place = {"x": [n], "y": [n + 3, n + 1], "z": [n + 4], "core": [n + 2]}
    axes = list(range(n)) + place["core"] + [a for dim in order for a in place[dim]] + [n + 5]
    return split.transpose(axes).reshape(array.shape)


def ring_first_stage(parts, where, perms, axes):
    dims = [order[0] for order in ORDERS]
    split = []
    for part in parts:
        rows, cols = part.shape
        quarter = part.reshape(4, 2, rows // 8, cols)
        split.append((quarter[:, 0], quarter[:, 1]))

    def own(block, index):
        return lax.dynamic_index_in_dim(block, index % 4, 0, keepdims=False)

    acc = [
        (own(ahead, where[dim] - 1), own(behind, where[dim] + 1))
        for dim, (ahead, behind) in zip(dims, split)
    ]
    for step in (2, 3, 4):
        moved = [
            (lax.ppermute(a, axes[dim], perms[dim][0]), lax.ppermute(b, axes[dim], perms[dim][1]))
            for dim, (a, b) in zip(dims, acc)
        ]
        moved = lax.optimization_barrier(moved)
        acc = [
            (a + own(ahead, where[dim] - step), b + own(behind, where[dim] + step))
            for dim, (a, b), (ahead, behind) in zip(dims, moved, split)
        ]
    return [jnp.concatenate(pair, axis=0) for pair in acc]


def reduce_colours(halves, where):
    perms, axes = reduction_plan(lax.axis_size("seg"), lax.axis_size("dp"))
    halves = lax.optimization_barrier(halves)
    parts = [keep + lax.ppermute(send, "seg", perms["core"]) for keep, send in halves]
    parts = ring_first_stage(parts, where, perms, axes)
    for stage in range(1, 3):
        groups = {}
        for color, order in enumerate(ORDERS):
            groups.setdefault(order[stage], []).append(color)
        moved = []
        for dim, members in groups.items():
            part = jnp.concatenate([parts[c] for c in members], axis=1)
            rows, cols = part.shape
            chunks = part.reshape(4, rows // 4, cols)

            def own(index, chunks=chunks):
                return lax.dynamic_index_in_dim(chunks, index % 4, 0, keepdims=False)

            coord = where[dim]
            sends = [
                lax.ppermute(own(coord + 1), axes[dim], perms[dim][0]),
                lax.ppermute(own(coord - 1), axes[dim], perms[dim][1]),
                lax.ppermute(own(coord + 2), axes[dim], perms[dim][2]),
            ]
            moved.append((own(coord), sends))
        moved = lax.optimization_barrier(moved)
        for members, (mine, sends) in zip(groups.values(), moved):
            total = mine + sends[0] + sends[1] + sends[2]
            edge = 0
            for c in members:
                width = parts[c].shape[1]
                parts[c] = total[:, edge : edge + width]
                edge += width
    return parts


def local(hidden, norm_gain, value_weight, queries, token_keys, summary_keys, output_grad):
    trace_count, row_count, value_width = queries.shape
    slot_count = summary_keys.shape[1]
    model_width = hidden.shape[2]
    mixing = mixing_of(queries, token_keys, summary_keys)
    grad_heads = output_grad.reshape(trace_count, row_count, HEADS, HEAD_DIM)
    direct = jnp.einsum("thrk,trhd->tkhd", mixing, grad_heads, preferred_element_type=jnp.float32)
    slot_mixing = mixing[:, :, row_count - slot_count :, :].astype(jnp.float32)
    own_map = jnp.swapaxes(slot_mixing[..., :slot_count], 2, 3)
    own_offset = direct[:, :slot_count]

    chain_map, chain_offset = own_map, own_offset
    offset, seg_size = 1, lax.axis_size("seg")
    while 2 * offset < seg_size:
        far_offset = passed_along(chain_offset, "seg", -offset)
        far_map = passed_along(chain_map, "seg", -offset)
        chain_offset = apply_map(chain_map, far_offset) + chain_offset
        chain_map = jnp.einsum(
            "thkm,thmr->thkr", chain_map, far_map, precision=lax.Precision.HIGHEST
        )
        offset *= 2
    past_half = passed_along(chain_offset, "seg", -offset)
    past_next_half = passed_along(chain_offset, "seg", -offset - 1)
    next_map = passed_along(chain_map, "seg", -1)
    next_offset = passed_along(chain_offset, "seg", -1)
    summary_state = apply_map(chain_map, past_half) + chain_offset
    incoming = apply_map(next_map, past_next_half) + next_offset
    summary_grad = summary_state.reshape(trace_count, slot_count, value_width)
    token_part = jnp.einsum(
        "thrk,trhd->tkhd", slot_mixing[..., slot_count:], incoming, precision=lax.Precision.HIGHEST
    )
    value_grad = (direct[:, slot_count:] + token_part).astype(jnp.bfloat16)
    value_grad = value_grad.reshape(trace_count * row_count, value_width)
    hidden_f = hidden.astype(jnp.float32)
    inv_rms = lax.rsqrt(jnp.mean(hidden_f * hidden_f, axis=-1, keepdims=True) + 1e-05)
    normed = hidden_f * inv_rms
    gain_f = norm_gain.astype(jnp.float32)
    scaled = (normed * gain_f).astype(jnp.bfloat16).reshape(trace_count * row_count, model_width)
    normalized_gradient = lax.dot_general(
        value_grad, value_weight, (((1,), (1,)), ((), ())), preferred_element_type=jnp.float32
    )
    normalized_gradient = normalized_gradient.reshape(trace_count, row_count, model_width)
    gain_grad = jnp.sum(
        (normalized_gradient * normed).reshape(trace_count * row_count, model_width), axis=0
    )
    scaled_grad = normalized_gradient * gain_f
    hidden_grad = inv_rms * (
        scaled_grad - normed * jnp.mean(scaled_grad * normed, axis=-1, keepdims=True)
    )
    seg_index, dp_index = lax.axis_index("seg"), lax.axis_index("dp")
    z_n = lax.axis_size("dp") // 2
    where = {
        "x": seg_index // 4,
        "y": 2 * (dp_index // z_n) + (seg_index // 2) % 2,
        "z": dp_index % z_n,
        "core": seg_index % 2,
    }
    seg_size, dp_size = lax.axis_size("seg"), lax.axis_size("dp")
    bounds = (0, 768, 1536, value_width)
    halves = []
    half = model_width // 2
    core = where["core"]
    for color, order in enumerate(ORDERS):
        columns = value_grad[:, bounds[color] : bounds[color + 1]]
        last = color == len(ORDERS) - 1
        if last:
            spare = jnp.zeros((columns.shape[0], 128), columns.dtype)
            columns = jnp.concatenate([columns, spare], axis=1)
            gain_col = feature_order(gain_grad, order, seg_size, dp_size)
        ordered = feature_order(scaled, order, seg_size, dp_size)
        pair = []
        for pick in (core, 1 - core):
            rows = lax.dynamic_slice_in_dim(ordered, pick * half, half, 1)
            part = lax.dot_general(
                rows, columns, (((0,), (0,)), ((), ())), preferred_element_type=jnp.float32
            )
            if last:
                lane = lax.broadcasted_iota(jnp.int32, part.shape, 1)
                gain_half = lax.dynamic_slice_in_dim(gain_col, pick * half, half, 0)
                gain_lane = part.shape[1] - 128
                part = part + jnp.where(lane == gain_lane, gain_half[:, None], jnp.float32(0))
            pair.append(part)
        halves.append(pair)
    pieces = reduce_colours(halves, where)
    both = jnp.concatenate(pieces, axis=1)
    weight_part, gain_part = both[:, :value_width], both[:, value_width]
    return (hidden_grad.astype(jnp.bfloat16), summary_grad, weight_part, gain_part)


def solution(mesh):
    placed = (
        P("dp", "seg", None),
        P(),
        P(),
        P("dp", "seg", None),
        P("dp", "seg", None),
        P("dp", "seg", None),
        P("dp", "seg", None),
    )
    return jax.shard_map(
        local,
        mesh=mesh,
        in_specs=placed,
        out_specs=(
            P("dp", "seg", None),
            P("dp", "seg", None),
            P(("seg", "dp"), None),
            P(("seg", "dp")),
        ),
        check_vma=False,
    )
```
